512 devices in a mesh: seq: 64 (over z, y), tp: 8 (over x, core).
Axes of the slice: x: 4, y: 4, z: 16, core: 2. Of those that a mesh axis runs over, the one named last changes fastest.
Arguments:
- queries: bfloat16 [64, 32, 4096], P('seq', None, 'tp'), may hold values from -15 to 15
- tree_keys: bfloat16 [64, 32, 1024], P('seq', None, 'tp'), may hold values from -15 to 15
- tree_values: bfloat16 [64, 32, 1024], P('seq', None, 'tp'), may hold values from -6 to 6
- cache_keys: bfloat16 [36864, 1024], P('seq', 'tp'), may hold values from -15 to 15
- cache_values: bfloat16 [36864, 1024], P('seq', 'tp'), may hold values from -6 to 6
- residual: bfloat16 [64, 32, 4096], P('seq', None, 'tp'), may hold values from -6 to 6
- out_weight: bfloat16 [4096, 4096], P('tp'), may hold values from -0.125 to 0.125
- cache_len: int32 [64], replicated, may hold values from 88 to 1720, as said below
- parents: int32 [64, 32], P('seq'), may hold values from -1 to 30, as said below
- accept_rows: int32 [64, 8], P('seq'), may hold values from 0 to 31, as said below
- accept_len: int32 [64], replicated, may hold values from 1 to 8
Outputs:
- mixed: bfloat16 [64, 32, 4096], P('seq', None, 'tp')
- new_cache_keys: bfloat16 [36864, 1024], P('seq', 'tp')
- new_cache_values: bfloat16 [36864, 1024], P('seq', 'tp')
The draws below stay inside these ranges and needn't reach their ends.
Inputs may be any that keep to these rules, and one draw needn't show every extreme that they name: Requests form aligned groups of 4 (requests 4 g to 4 g + 3). Request r owns cache_len[r] + 8 pool positions, these regions follow one another in request order from position 0, and the regions of one group fill exactly 2304 positions, so that group g's caches lie in pool positions 4 * 576 * g to 4 * 576 * (g + 1) - 1. parents[r, 0] = -1, and 0 <= parents[r, i] < i for i > 0. `accept_rows`: entries 0 to accept_len[r] - 1 are a chain of tree tokens that starts at token 0, each entry's parent being the entry before it; later entries are 31 and are not used.
All inputs are finite; a program needn't handle non-finite values.
Results may differ from the reference program's by a relative error of at most 0.009.
Values may be sent and summed in bfloat16 or wider, within the bound.
No kernel may reach another device: no remote copies, remote signals or barrier semaphores. Data moves between devices by JAX's collectives and lax.ppermute only.
A program may use at most 64 MiB of HBM per device.

```python
import math
import jax
import jax.numpy as jnp
from jax import lax

D = 4096
HQ = 32
KVH = 8
HD = 128
TREE = 32
A_MAX = 8
GROUP = 4
P_DEV = 576
REQS = 64
POOL = 36864


def drawn_rows(key, leading, heads, salt):
    drawn = jnp.clip(jax.random.normal(jax.random.fold_in(key, salt), leading + (heads, HD), jnp.float32), -6.0, 6.0)
    return drawn.reshape(leading + (heads * HD,))


def draw_queries(key, part):
    values = drawn_rows(key, (REQS, TREE), HQ, 31)
    return values.astype(jnp.bfloat16)


def draw_tree_keys(key, part):
    values = drawn_rows(key, (REQS, TREE), KVH, 41)
    return values.astype(jnp.bfloat16)


def draw_cache_keys(key, part):
    values = drawn_rows(key, (P_DEV * REQS,), KVH, 51)
    return values.astype(jnp.bfloat16)


def draw_cache_len(key, part):
    groups = REQS // GROUP
    long_at = jax.random.randint(jax.random.fold_in(key, 11), (groups, 1), 0, GROUP)
    third = P_DEV // 3
    stride = P_DEV // 12
    first_shift = jax.random.randint(jax.random.fold_in(key, 12), (groups,), -stride, stride + 1)
    second_shift = jax.random.randint(jax.random.fold_in(key, 13), (groups,), -stride, stride + 1)
    picked = jax.random.randint(jax.random.fold_in(key, 14), (), 0, groups)
    group_ids = jnp.arange(groups, dtype=jnp.int32)
    first_shift = jnp.where(group_ids == picked, stride, first_shift)
    second_shift = jnp.where(group_ids == picked, -stride, second_shift)
    shorts = jnp.stack([third + first_shift, third - first_shift + second_shift, third - second_shift], axis=1)
    slots = jnp.arange(GROUP, dtype=jnp.int32)[None, :]
    short_index = jnp.clip(slots - (slots > long_at).astype(jnp.int32), 0, 2)
    short_value = jnp.take_along_axis(shorts, jnp.broadcast_to(short_index, (groups, GROUP)), axis=1)
    regions = jnp.where(slots == long_at, (GROUP - 1) * P_DEV, short_value)
    return (regions - A_MAX).reshape(-1).astype(jnp.int32)


def tree_layout(key):
    members = jnp.arange(TREE, dtype=jnp.int32)
    lowest = jnp.maximum(members - 3, 0)
    highest = jnp.maximum(members, 1)
    parent_ids = jax.random.randint(jax.random.fold_in(key, 21), (REQS, TREE), lowest, highest)
    parent_ids = jnp.where(members[None, :] == 0, -1, parent_ids).astype(jnp.int32)
    parent_ids = parent_ids.at[0, TREE - 1].set(TREE - 2)
    endings = jax.random.randint(jax.random.fold_in(key, 22), (REQS,), 0, TREE)
    order = jax.random.permutation(jax.random.fold_in(key, 23), REQS)
    endings = endings.at[order[0]].set(0).at[order[1]].set(TREE - 1)
    current = endings.astype(jnp.int32)
    links = [current]
    for repeat in range(TREE - 1):
        hopped = jnp.take_along_axis(parent_ids, jnp.maximum(current, 0)[:, None], axis=1)[:, 0]
        current = jnp.where(current >= 0, hopped, -1)
        links.append(current)
    chain = jnp.stack(links, axis=1)
    depth = jnp.sum((chain >= 0).astype(jnp.int32), axis=1) - 1
    counts = jnp.minimum(depth + 1, A_MAX).astype(jnp.int32)
    column = jnp.arange(A_MAX, dtype=jnp.int32)
    picks = jnp.maximum(depth[:, None] - column[None, :], 0)
    path_rows = jnp.take_along_axis(chain, picks, axis=1)
    path_rows = jnp.where(column[None, :] < counts[:, None], path_rows, TREE - 1).astype(jnp.int32)
    return (parent_ids, path_rows, counts)


def draw_parents(key, part):
    return tree_layout(jax.random.fold_in(key, 77))[0]


def draw_accept_rows(key, part):
    return tree_layout(jax.random.fold_in(key, 77))[1]


def draw_accept_len(key, part):
    return tree_layout(jax.random.fold_in(key, 77))[2]


def with_spikes(result, stream_key, source, target, parts, factor):
    def block_of(axis_at):
        return (jnp.arange(result.shape[axis_at]) // (result.shape[axis_at] // parts)).reshape((-1,) + (1,) * (result.ndim - 1 - axis_at))

    first = jax.random.permutation(stream_key, parts)[block_of(target)]
    second = (block_of(target) + parts // 2) % parts
    return jnp.where((block_of(source) == first) | (block_of(source) == second), factor * result, result)


def steps_of(key, extent, split, low, top_value):
    def one(dim, shards_of):
        steps = jax.random.uniform(jax.random.fold_in(jax.random.fold_in(key, 6), dim), (shards_of,), jnp.float32, low / len(split), top_value / len(split))
        return jnp.repeat(jnp.exp(steps), extent[dim] // shards_of).reshape((-1,) + (1,) * (len(extent) - dim - 1))

    loudness = one(*split[0])
    for cut in split[1:]:
        loudness = loudness * one(*cut)
    return loudness


def centred(own_key, shape, width, bound, cuts=(), kind=jnp.bfloat16):
    drawn = jax.random.normal(own_key, shape, jnp.float32) * width
    if len(cuts) > 0:
        drawn = steps_of(own_key, shape, cuts, -0.22, 0.18) * drawn
    return jnp.clip(drawn, min=-bound, max=bound).astype(kind)


def bell_draw_with(rng, dims, deviation, limit, split, heavy, kind=jnp.bfloat16):
    values = deviation * jax.random.normal(rng, dims, jnp.float32)
    if split:
        values = values * steps_of(rng, dims, split, -0.22, 0.18)
    return jnp.clip(with_spikes(values, jax.random.fold_in(rng, 3), *heavy), -limit, limit).astype(kind)


def setup_inputs(seed: int = 0) -> dict:
    arg_keys = jax.random.split(jax.random.key(seed), 12)
    queries = draw_queries(jax.random.fold_in(arg_keys[11], 71), 0)
    tree_keys = draw_tree_keys(jax.random.fold_in(arg_keys[11], 71), 0)
    tree_values = centred(arg_keys[2], (REQS, TREE, KVH * HD), 1.0, 6.0, ((0, 64), (2, 8)))
    cache_keys = draw_cache_keys(jax.random.fold_in(arg_keys[11], 71), 0)
    cache_values = centred(arg_keys[4], (POOL, KVH * HD), 1.0, 6.0, ((0, 64), (1, 8)))
    residual = centred(arg_keys[5], (REQS, TREE, D), 1.0, 6.0, ((0, 64), (2, 8)))
    out_weight = bell_draw_with(arg_keys[6], (HQ * HD, D), (HQ * HD) ** -0.5, 0.125, ((0, 8),), (0, 1, 8, 2.0))
    cache_len = draw_cache_len(jax.random.fold_in(arg_keys[11], 71), 0)
    parents = draw_parents(jax.random.fold_in(arg_keys[11], 71), 0)
    accept_rows = draw_accept_rows(jax.random.fold_in(arg_keys[11], 71), 0)
    accept_len = draw_accept_len(jax.random.fold_in(arg_keys[11], 71), 0)
    return {"queries": queries, "tree_keys": tree_keys, "tree_values": tree_values, "cache_keys": cache_keys, "cache_values": cache_values, "residual": residual, "out_weight": out_weight, "cache_len": cache_len, "parents": parents, "accept_rows": accept_rows, "accept_len": accept_len}


NEG = -1e+30

def ancestry(parents):
    length = parents.shape[-1]
    members = jnp.arange(length, dtype=jnp.int32)
    ancestors = jnp.broadcast_to(members[:, None] == members[None, :], parents.shape + (length,))
    current = parents
    for repeat in range(length - 1):
        ancestors = ancestors | (current[..., None] == members)
        hopped = jnp.take_along_axis(parents, jnp.maximum(current, 0), axis=-1)
        current = jnp.where(current >= 0, hopped, -1)
    return ancestors

def reference(queries, tree_keys, tree_values, cache_keys, cache_values, residual, out_weight, cache_len, parents, accept_rows, accept_len):
    pool_size = cache_keys.shape[0]
    window = min(GROUP * P_DEV, pool_size)
    regions = cache_len + A_MAX
    starts = (jnp.cumsum(regions) - regions).astype(jnp.int32)
    ancestors = ancestry(parents)
    sharing = HQ // KVH
    factor = 1.0 / math.sqrt(HD)
    highest = lax.Precision.HIGHEST

    def attend(request):
        query_rows = queries[request].reshape(TREE, KVH, sharing, HD).astype(jnp.float32)
        begin = starts[request]
        length = cache_len[request]
        offset = jnp.minimum(begin, pool_size - window).astype(jnp.int32)
        keys_win = lax.dynamic_slice_in_dim(cache_keys, offset, window, 0).reshape(window, KVH, HD).astype(jnp.float32)
        values_win = lax.dynamic_slice_in_dim(cache_values, offset, window, 0).reshape(window, KVH, HD).astype(jnp.float32)
        places = offset + jnp.arange(window, dtype=jnp.int32)
        inside = (places >= begin) & (places < begin + length)
        cached = jnp.einsum('tkgd,pkd->kgtp', query_rows, keys_win, precision=highest) * factor
        own_keys = tree_keys[request].reshape(TREE, KVH, HD).astype(jnp.float32)
        own_values = tree_values[request].reshape(TREE, KVH, HD).astype(jnp.float32)
        drafted = jnp.einsum('tkgd,jkd->kgtj', query_rows, own_keys, precision=highest) * factor
        linked = ancestors[request]
        top = jnp.maximum(lax.optimization_barrier(jnp.max(jnp.where(inside, cached, NEG), axis=-1)), lax.optimization_barrier(jnp.max(jnp.where(linked, drafted, NEG), axis=-1)))
        cache_raised = jnp.where(inside, jnp.exp(cached - top[..., None]), 0.0)
        tree_raised = jnp.where(linked, jnp.exp(drafted - top[..., None]), 0.0)
        total = lax.optimization_barrier(jnp.sum(cache_raised, axis=-1)) + lax.optimization_barrier(jnp.sum(tree_raised, axis=-1))
        cache_weights = lax.optimization_barrier(cache_raised.astype(jnp.bfloat16)).astype(jnp.float32)
        tree_weights = lax.optimization_barrier(tree_raised.astype(jnp.bfloat16)).astype(jnp.float32)
        summed = jnp.einsum('kgtp,pkd->tkgd', cache_weights, values_win, precision=highest)
        summed = summed + jnp.einsum('kgtj,jkd->tkgd', tree_weights, own_values, precision=highest)
        scaled = summed / jnp.transpose(total, (2, 0, 1))[..., None]
        return scaled.astype(jnp.bfloat16).reshape(TREE, HQ * HD)
    attention = lax.map(attend, jnp.arange(REQS, dtype=jnp.int32))
    projected = jnp.dot(attention.reshape(REQS * TREE, HQ * HD), out_weight, preferred_element_type=jnp.float32)
    mixed = (residual.astype(jnp.float32) + projected.reshape(REQS, TREE, D)).astype(jnp.bfloat16)
    column = jnp.arange(A_MAX, dtype=jnp.int32)
    targets = starts[:, None] + cache_len[:, None] + column[None, :]
    targets = jnp.where(column[None, :] < accept_len[:, None], targets, pool_size).reshape(-1).astype(jnp.int32)
    key_rows = jnp.take_along_axis(tree_keys, accept_rows[:, :, None], axis=1).reshape(-1, KVH * HD)
    value_rows = jnp.take_along_axis(tree_values, accept_rows[:, :, None], axis=1).reshape(-1, KVH * HD)
    new_cache_keys = cache_keys.at[targets].set(key_rows, mode='drop')
    new_cache_values = cache_values.at[targets].set(value_rows, mode='drop')
    return (mixed, new_cache_keys, new_cache_values)
```

```python
import math

import jax
import jax.numpy as jnp
import numpy as np
from jax import lax
from jax.sharding import Mesh
from jax.sharding import PartitionSpec as P

HD = 128
TREE = 32
A_MAX = 8
GROUP = 4


NEG = -1e30


def ancestry(parents):
    length = parents.shape[-1]
    members = jnp.arange(length, dtype=jnp.int32)
    step = (members[:, None] == members[None, :]) | (parents[:, None] == members[None, :])
    reach = step.astype(jnp.bfloat16)
    covered = 1
    while covered < length - 1:
        reach = (
            jnp.dot(reach, reach, preferred_element_type=jnp.float32) > 0
        ).astype(jnp.bfloat16)
        covered *= 2
    return reach > 0


def scale_heads(values, factors):
    return (values.reshape(factors.shape + (HD,)) * factors[..., None]).reshape(values.shape)


def on_device(
    queries,
    tree_keys,
    tree_values,
    cache_keys,
    cache_values,
    residual,
    out_weight,
    cache_len,
    parents,
    accept_rows,
    accept_len,
):
    member = lax.axis_index("mem")
    seq_rank = lax.axis_index("grp") * GROUP + member
    positions = cache_keys.shape[0]
    channels = cache_keys.shape[1]
    kv_local = channels // HD
    q_width = queries.shape[2]
    heads_local = q_width // HD
    sharing = heads_local // kv_local
    factor = 1.0 / math.sqrt(HD)
    regions = cache_len + A_MAX
    starts = jnp.cumsum(regions) - regions
    low_edge = seq_rank * positions
    places = low_edge + jnp.arange(positions, dtype=jnp.int32)
    keys_local = cache_keys.reshape(positions, kv_local, HD)
    values_local = cache_values.reshape(positions, kv_local, HD)

    tree_pair = jnp.concatenate([tree_keys[0], tree_values[0]], axis=-1)
    mine_rows = jnp.take(tree_pair, accept_rows[0], axis=0)
    q_size = TREE * q_width
    packed = jnp.concatenate([queries[0].reshape(-1), mine_rows.reshape(-1)])
    sent = jnp.broadcast_to(packed[None], (GROUP, packed.shape[0]))
    got = lax.all_to_all(sent, "mem", 0, 0, tiled=True)
    gathered_q = got[:, :q_size].reshape(GROUP, TREE, q_width)
    row_block = got[:, q_size:].reshape(GROUP, A_MAX, 2 * channels)

    group_base = seq_rank - member
    begin = lax.dynamic_slice_in_dim(starts, group_base, GROUP)
    length = lax.dynamic_slice_in_dim(cache_len, group_base, GROUP)
    inside = (places[None, :] >= begin[:, None]) & (places[None, :] < (begin + length)[:, None])
    shaped = gathered_q.reshape(GROUP, TREE, kv_local, sharing, HD)
    scores = (
        jnp.einsum("rtkgd,pkd->rkgtp", shaped, keys_local, preferred_element_type=jnp.float32)
        * factor
    )
    valid = inside[:, None, None, None, :]
    top_score = jnp.max(jnp.where(valid, scores, NEG), axis=-1)
    raised = jnp.where(valid, jnp.exp(scores - top_score[..., None]), 0.0)
    total = jnp.sum(raised, axis=-1)
    summed = jnp.einsum(
        "rkgtp,pkd->rtkgd",
        raised.astype(jnp.bfloat16),
        values_local,
        preferred_element_type=jnp.float32,
    )
    top_rows = jnp.transpose(top_score, (0, 3, 1, 2)).reshape(GROUP, TREE, heads_local)
    total_rows = jnp.transpose(total, (0, 3, 1, 2)).reshape(GROUP, TREE, heads_local)
    partial = jnp.concatenate(
        [summed.reshape(GROUP, TREE, q_width), top_rows, total_rows], axis=-1
    )
    partials = lax.all_to_all(partial, "mem", 0, 0, tiled=True)
    part_out = partials[:, :, :q_width]
    part_top = partials[:, :, q_width : q_width + heads_local]
    part_total = partials[:, :, q_width + heads_local :]

    linked = ancestry(parents[0])
    shaped_q = queries[0].reshape(TREE, kv_local, sharing, HD)
    own_keys = tree_keys[0].reshape(TREE, kv_local, HD)
    own_values = tree_values[0].reshape(TREE, kv_local, HD)
    drafted = (
        jnp.einsum("tkgd,jkd->kgtj", shaped_q, own_keys, preferred_element_type=jnp.float32)
        * factor
    )
    tree_top = jnp.max(jnp.where(linked, drafted, NEG), axis=-1)
    tree_raised = jnp.where(linked, jnp.exp(drafted - tree_top[..., None]), 0.0)
    tree_total = jnp.sum(tree_raised, axis=-1)
    tree_out = jnp.einsum(
        "kgtj,jkd->tkgd",
        tree_raised.astype(jnp.bfloat16),
        own_values,
        preferred_element_type=jnp.float32,
    ).reshape(TREE, q_width)
    tree_top = jnp.transpose(tree_top, (2, 0, 1)).reshape(TREE, heads_local)
    tree_total = jnp.transpose(tree_total, (2, 0, 1)).reshape(TREE, heads_local)

    joint_top = jnp.maximum(jnp.max(part_top, axis=0), tree_top)
    part_factor = jnp.exp(part_top - joint_top[None])
    tree_factor = jnp.exp(tree_top - joint_top)
    joint_out = jnp.sum(scale_heads(part_out, part_factor), axis=0) + scale_heads(
        tree_out, tree_factor
    )
    joint_total = jnp.sum(part_total * part_factor, axis=0) + tree_total * tree_factor
    attention = scale_heads(joint_out, 1.0 / joint_total).astype(jnp.bfloat16)

    tp_size = lax.axis_size("tp")
    projected = jnp.dot(attention, out_weight, preferred_element_type=jnp.float32).astype(
        jnp.bfloat16
    )
    pieces = jnp.transpose(projected.reshape(TREE, tp_size, -1), (1, 0, 2))
    pieces = lax.all_to_all(pieces, "tp", 0, 0, tiled=True)
    summed_heads = jnp.sum(pieces.astype(jnp.float32), axis=0)
    mixed = (residual[0].astype(jnp.float32) + summed_heads).astype(jnp.bfloat16)[None]

    row_accepted = lax.dynamic_slice_in_dim(accept_len, group_base, GROUP)
    column = jnp.arange(A_MAX, dtype=jnp.int32)
    targets = begin[:, None] + length[:, None] + column[None, :] - low_edge
    keep_row = (column[None, :] < row_accepted[:, None]) & (targets >= 0) & (targets < positions)
    targets = jnp.where(keep_row, targets, positions).reshape(-1)
    rows = row_block.reshape(-1, 2 * channels)
    new_keys = cache_keys.at[targets].set(rows[:, :channels], mode="drop")
    new_values = cache_values.at[targets].set(rows[:, channels:], mode="drop")
    return (mixed, new_keys, new_values)


def solution(mesh):
    seq_size = mesh.shape["seq"]
    tp_size = mesh.shape["tp"]
    devices = np.asarray(mesh.devices).reshape(seq_size // GROUP, GROUP, tp_size)
    inner = Mesh(devices, ("grp", "mem", "tp"))
    seq = ("grp", "mem")
    return jax.shard_map(
        on_device,
        mesh=inner,
        in_specs=(
            P(seq, None, "tp"),
            P(seq, None, "tp"),
            P(seq, None, "tp"),
            P(seq, "tp"),
            P(seq, "tp"),
            P(seq, None, "tp"),
            P("tp", None),
            P(),
            P(seq, None),
            P(seq, None),
            P(),
        ),
        out_specs=(P(seq, None, "tp"), P(seq, "tp"), P(seq, "tp")),
        check_vma=False,
    )
```

```python
import math

import jax
import jax.numpy as jnp
import numpy as np
from jax import lax
from jax.sharding import Mesh
from jax.sharding import PartitionSpec as P

HD = 128
TREE = 32
A_MAX = 8
GROUP = 4


NEG = -1e30


def ancestry(parents):
    length = parents.shape[-1]
    members = jnp.arange(length, dtype=jnp.int32)
    step = (members[:, None] == members[None, :]) | (parents[:, None] == members[None, :])
    reach = step.astype(jnp.bfloat16)
    covered = 1
    while covered < length - 1:
        reach = (
            jnp.dot(reach, reach, preferred_element_type=jnp.float32) > 0
        ).astype(jnp.bfloat16)
        covered *= 2
    return reach > 0


def scale_heads(values, factors):
    return (values.reshape(factors.shape + (HD,)) * factors[..., None]).reshape(values.shape)


def on_device(
    queries,
    tree_keys,
    tree_values,
    cache_keys,
    cache_values,
    residual,
    out_weight,
    cache_len,
    parents,
    accept_rows,
    accept_len,
):
    member = lax.axis_index("mem")
    seq_rank = lax.axis_index("grp") * GROUP + member
    positions = cache_keys.shape[0]
    channels = cache_keys.shape[1]
    kv_local = channels // HD
    q_width = queries.shape[2]
    heads_local = q_width // HD
    sharing = heads_local // kv_local
    factor = 1.0 / math.sqrt(HD)
    regions = cache_len + A_MAX
    starts = jnp.cumsum(regions) - regions
    low_edge = seq_rank * positions
    places = low_edge + jnp.arange(positions, dtype=jnp.int32)
    keys_local = cache_keys.reshape(positions, kv_local, HD)
    values_local = cache_values.reshape(positions, kv_local, HD)

    sent = jnp.broadcast_to(queries, (GROUP,) + queries.shape[1:])
    gathered_q = lax.all_to_all(sent, "mem", 0, 0, tiled=True)

    group_base = seq_rank - member
    begin = lax.dynamic_slice_in_dim(starts, group_base, GROUP)
    length = lax.dynamic_slice_in_dim(cache_len, group_base, GROUP)
    inside = (places[None, :] >= begin[:, None]) & (places[None, :] < (begin + length)[:, None])
    shaped = gathered_q.reshape(GROUP, TREE, kv_local, sharing, HD)
    scores = (
        jnp.einsum("rtkgd,pkd->rkgtp", shaped, keys_local, preferred_element_type=jnp.float32)
        * factor
    )
    valid = inside[:, None, None, None, :]
    top_score = jnp.max(jnp.where(valid, scores, NEG), axis=-1)
    raised = jnp.where(valid, jnp.exp(scores - top_score[..., None]), 0.0)
    total = jnp.sum(raised, axis=-1)
    summed = jnp.einsum(
        "rkgtp,pkd->rtkgd",
        raised.astype(jnp.bfloat16),
        values_local,
        preferred_element_type=jnp.float32,
    )
    top_rows = jnp.transpose(top_score, (0, 3, 1, 2)).reshape(GROUP, TREE, heads_local)
    total_rows = jnp.transpose(total, (0, 3, 1, 2)).reshape(GROUP, TREE, heads_local)
    partial = jnp.concatenate(
        [summed.reshape(GROUP, TREE, q_width), top_rows, total_rows], axis=-1
    )
    tree_pair = jnp.concatenate([tree_keys[0], tree_values[0]], axis=-1)
    mine_rows = jnp.take(tree_pair, accept_rows[0], axis=0).astype(jnp.float32)
    width = partial.shape[-1]
    row_lines = mine_rows.reshape(-1, q_width)
    row_lines = jnp.pad(row_lines, ((0, 0), (0, width - q_width)))
    row_lines = jnp.broadcast_to(row_lines[None], (GROUP,) + row_lines.shape)
    message = jnp.concatenate([partial, row_lines], axis=1)
    partials = lax.all_to_all(message, "mem", 0, 0, tiled=True)
    row_block = partials[:, TREE:, :q_width].reshape(GROUP, A_MAX, 2 * channels)
    row_block = row_block.astype(jnp.bfloat16)
    partials = partials[:, :TREE]
    part_out = partials[:, :, :q_width]
    part_top = partials[:, :, q_width : q_width + heads_local]
    part_total = partials[:, :, q_width + heads_local :]

    linked = ancestry(parents[0])
    shaped_q = queries[0].reshape(TREE, kv_local, sharing, HD)
    own_keys = tree_keys[0].reshape(TREE, kv_local, HD)
    own_values = tree_values[0].reshape(TREE, kv_local, HD)
    drafted = (
        jnp.einsum("tkgd,jkd->kgtj", shaped_q, own_keys, preferred_element_type=jnp.float32)
        * factor
    )
    tree_top = jnp.max(jnp.where(linked, drafted, NEG), axis=-1)
    tree_raised = jnp.where(linked, jnp.exp(drafted - tree_top[..., None]), 0.0)
    tree_total = jnp.sum(tree_raised, axis=-1)
    tree_out = jnp.einsum(
        "kgtj,jkd->tkgd",
        tree_raised.astype(jnp.bfloat16),
        own_values,
        preferred_element_type=jnp.float32,
    ).reshape(TREE, q_width)
    tree_top = jnp.transpose(tree_top, (2, 0, 1)).reshape(TREE, heads_local)
    tree_total = jnp.transpose(tree_total, (2, 0, 1)).reshape(TREE, heads_local)

    joint_top = jnp.maximum(jnp.max(part_top, axis=0), tree_top)
    part_factor = jnp.exp(part_top - joint_top[None])
    tree_factor = jnp.exp(tree_top - joint_top)
    joint_out = jnp.sum(scale_heads(part_out, part_factor), axis=0) + scale_heads(
        tree_out, tree_factor
    )
    joint_total = jnp.sum(part_total * part_factor, axis=0) + tree_total * tree_factor
    attention = scale_heads(joint_out, 1.0 / joint_total).astype(jnp.bfloat16)

    tp_size = lax.axis_size("tp")
    projected = lax.dot_general(
        out_weight, attention, (((0,), (1,)), ((), ())), preferred_element_type=jnp.float32
    ).astype(jnp.bfloat16)
    pieces = projected.reshape(tp_size, -1, TREE)
    pieces = lax.all_to_all(pieces, "tp", 0, 0, tiled=True)
    summed_heads = jnp.sum(pieces.astype(jnp.float32), axis=0)
    mixed = (residual[0].astype(jnp.float32) + summed_heads.T).astype(jnp.bfloat16)[None]

    row_accepted = lax.dynamic_slice_in_dim(accept_len, group_base, GROUP)
    column = jnp.arange(A_MAX, dtype=jnp.int32)
    targets = begin[:, None] + length[:, None] + column[None, :] - low_edge
    keep_row = (column[None, :] < row_accepted[:, None]) & (targets >= 0) & (targets < positions)
    targets = jnp.where(keep_row, targets, positions).reshape(-1)
    rows = row_block.reshape(-1, 2 * channels)
    new_keys = cache_keys.at[targets].set(rows[:, :channels], mode="drop")
    new_values = cache_values.at[targets].set(rows[:, channels:], mode="drop")
    return (mixed, new_keys, new_values)


def solution(mesh):
    seq_size = mesh.shape["seq"]
    tp_size = mesh.shape["tp"]
    devices = np.asarray(mesh.devices).reshape(seq_size // GROUP, GROUP, tp_size)
    inner = Mesh(devices, ("grp", "mem", "tp"))
    seq = ("grp", "mem")
    return jax.shard_map(
        on_device,
        mesh=inner,
        in_specs=(
            P(seq, None, "tp"),
            P(seq, None, "tp"),
            P(seq, None, "tp"),
            P(seq, "tp"),
            P(seq, "tp"),
            P(seq, None, "tp"),
            P("tp", None),
            P(),
            P(seq, None),
            P(seq, None),
            P(),
        ),
        out_specs=(P(seq, None, "tp"), P(seq, "tp"), P(seq, "tp")),
        check_vma=False,
    )
```

```python
import math

import jax
import jax.numpy as jnp
import numpy as np
from jax import lax
from jax.experimental import pallas as pl
from jax.sharding import Mesh
from jax.sharding import PartitionSpec as P

HD = 128
TREE = 32
A_MAX = 8
GROUP = 4


NEG = -1e30


def ancestry(parents):
    length = parents.shape[-1]
    members = jnp.arange(length, dtype=jnp.int32)
    step = (members[:, None] == members[None, :]) | (parents[:, None] == members[None, :])
    reach = step.astype(jnp.bfloat16)
    covered = 1
    while covered < length - 1:
        reach = (
            jnp.dot(reach, reach, preferred_element_type=jnp.float32) > 0
        ).astype(jnp.bfloat16)
        covered *= 2
    return reach > 0


def project_kernel(attention_ref, weight_ref, out_ref):
    result = jnp.dot(attention_ref[...], weight_ref[...], preferred_element_type=jnp.float32)
    width = out_ref.shape[2]
    for piece in range(out_ref.shape[0]):
        out_ref[piece] = result[:, piece * width : (piece + 1) * width].astype(out_ref.dtype)


def project(attention, weight, pieces):
    rows, cols = weight.shape
    width = cols // pieces
    per_step = 2 if pieces % 2 == 0 else 1
    return pl.pallas_call(
        project_kernel,
        grid=(pieces // per_step,),
        in_specs=[
            pl.BlockSpec((attention.shape[0], rows), lambda j: (0, 0)),
            pl.BlockSpec((rows, width * per_step), lambda j: (0, j)),
        ],
        out_specs=pl.BlockSpec((per_step, attention.shape[0], width), lambda j: (j, 0, 0)),
        out_shape=jax.ShapeDtypeStruct((pieces, attention.shape[0], width), jnp.bfloat16),
    )(attention, weight)


def scale_heads(values, factors):
    return (values.reshape(factors.shape + (HD,)) * factors[..., None]).reshape(values.shape)


def on_device(
    queries,
    tree_keys,
    tree_values,
    cache_keys,
    cache_values,
    residual,
    out_weight,
    cache_len,
    parents,
    accept_rows,
    accept_len,
):
    member = lax.axis_index("mem")
    seq_rank = lax.axis_index("grp") * GROUP + member
    positions = cache_keys.shape[0]
    channels = cache_keys.shape[1]
    kv_local = channels // HD
    q_width = queries.shape[2]
    heads_local = q_width // HD
    sharing = heads_local // kv_local
    factor = 1.0 / math.sqrt(HD)
    regions = cache_len + A_MAX
    starts = jnp.cumsum(regions) - regions
    low_edge = seq_rank * positions
    places = low_edge + jnp.arange(positions, dtype=jnp.int32)
    keys_local = cache_keys.reshape(positions, kv_local, HD)
    values_local = cache_values.reshape(positions, kv_local, HD)

    sent = jnp.broadcast_to(queries, (GROUP,) + queries.shape[1:])
    gathered_q = lax.all_to_all(sent, "mem", 0, 0, tiled=True)

    group_base = seq_rank - member
    begin = lax.dynamic_slice_in_dim(starts, group_base, GROUP)
    length = lax.dynamic_slice_in_dim(cache_len, group_base, GROUP)
    inside = (places[None, :] >= begin[:, None]) & (places[None, :] < (begin + length)[:, None])
    shaped = gathered_q.reshape(GROUP, TREE, kv_local, sharing, HD)
    scores = (
        jnp.einsum("rtkgd,pkd->rkgtp", shaped, keys_local, preferred_element_type=jnp.float32)
        * factor
    )
    valid = inside[:, None, None, None, :]
    top_score = jnp.max(jnp.where(valid, scores, NEG), axis=-1)
    raised = jnp.where(valid, jnp.exp(scores - top_score[..., None]), 0.0)
    total = jnp.sum(raised, axis=-1)
    summed = jnp.einsum(
        "rkgtp,pkd->rtkgd",
        raised.astype(jnp.bfloat16),
        values_local,
        preferred_element_type=jnp.float32,
    )
    stats = jnp.concatenate(
        [top_score.reshape(GROUP, 1, -1), total.reshape(GROUP, 1, -1)], axis=-1
    )
    stats = jnp.pad(stats, ((0, 0), (0, 0), (0, q_width - stats.shape[-1])))
    tree_pair = jnp.concatenate([tree_keys[0], tree_values[0]], axis=-1)
    mine_rows = jnp.take(tree_pair, accept_rows[0], axis=0).astype(jnp.float32)
    row_lines = mine_rows.reshape(1, -1, q_width)
    row_count = row_lines.shape[1]
    row_lines = jnp.broadcast_to(row_lines, (GROUP,) + row_lines.shape[1:])
    used = TREE + 1 + row_count
    filler = jnp.zeros((GROUP, -used % 8, q_width), jnp.float32)
    message = jnp.concatenate(
        [summed.reshape(GROUP, TREE, q_width), stats, row_lines, filler], axis=1
    )
    partials = lax.all_to_all(message, "mem", 0, 0, tiled=True)
    row_block = partials[:, TREE + 1 : used].reshape(GROUP, A_MAX, 2 * channels)
    row_block = row_block.astype(jnp.bfloat16)
    part_out = partials[:, :TREE]
    stat_count = kv_local * sharing * TREE
    part_stats = partials[:, TREE, : 2 * stat_count].reshape(GROUP, 2, heads_local, TREE)
    part_top = jnp.transpose(part_stats[:, 0], (0, 2, 1))
    part_total = jnp.transpose(part_stats[:, 1], (0, 2, 1))

    linked = ancestry(parents[0])
    shaped_q = queries[0].reshape(TREE, kv_local, sharing, HD)
    own_keys = tree_keys[0].reshape(TREE, kv_local, HD)
    own_values = tree_values[0].reshape(TREE, kv_local, HD)
    drafted = (
        jnp.einsum("tkgd,jkd->kgtj", shaped_q, own_keys, preferred_element_type=jnp.float32)
        * factor
    )
    tree_top = jnp.max(jnp.where(linked, drafted, NEG), axis=-1)
    tree_raised = jnp.where(linked, jnp.exp(drafted - tree_top[..., None]), 0.0)
    tree_total = jnp.sum(tree_raised, axis=-1)
    tree_out = jnp.einsum(
        "kgtj,jkd->tkgd",
        tree_raised.astype(jnp.bfloat16),
        own_values,
        preferred_element_type=jnp.float32,
    ).reshape(TREE, q_width)
    tree_top = jnp.transpose(tree_top, (2, 0, 1)).reshape(TREE, heads_local)
    tree_total = jnp.transpose(tree_total, (2, 0, 1)).reshape(TREE, heads_local)

    joint_top = jnp.maximum(jnp.max(part_top, axis=0), tree_top)
    part_factor = jnp.exp(part_top - joint_top[None])
    tree_factor = jnp.exp(tree_top - joint_top)
    joint_out = jnp.sum(scale_heads(part_out, part_factor), axis=0) + scale_heads(
        tree_out, tree_factor
    )
    joint_total = jnp.sum(part_total * part_factor, axis=0) + tree_total * tree_factor
    attention = scale_heads(joint_out, 1.0 / joint_total).astype(jnp.bfloat16)

    tp_size = lax.axis_size("tp")
    pieces = project(attention, out_weight, tp_size)
    pieces = lax.all_to_all(pieces, "tp", 0, 0, tiled=True)
    summed_heads = jnp.sum(pieces.astype(jnp.float32), axis=0)
    mixed = (residual[0].astype(jnp.float32) + summed_heads).astype(jnp.bfloat16)[None]

    row_accepted = lax.dynamic_slice_in_dim(accept_len, group_base, GROUP)
    column = jnp.arange(A_MAX, dtype=jnp.int32)
    targets = begin[:, None] + length[:, None] + column[None, :] - low_edge
    keep_row = (column[None, :] < row_accepted[:, None]) & (targets >= 0) & (targets < positions)
    targets = jnp.where(keep_row, targets, positions).reshape(-1)
    rows = row_block.reshape(-1, 2 * channels)
    new_keys = cache_keys.at[targets].set(rows[:, :channels], mode="drop")
    new_values = cache_values.at[targets].set(rows[:, channels:], mode="drop")
    return (mixed, new_keys, new_values)


def solution(mesh):
    seq_size = mesh.shape["seq"]
    tp_size = mesh.shape["tp"]
    devices = np.asarray(mesh.devices).reshape(seq_size // GROUP, GROUP, tp_size)
    inner = Mesh(devices, ("grp", "mem", "tp"))
    seq = ("grp", "mem")
    return jax.shard_map(
        on_device,
        mesh=inner,
        in_specs=(
            P(seq, None, "tp"),
            P(seq, None, "tp"),
            P(seq, None, "tp"),
            P(seq, "tp"),
            P(seq, "tp"),
            P(seq, None, "tp"),
            P("tp", None),
            P(),
            P(seq, None),
            P(seq, None),
            P(),
        ),
        out_specs=(P(seq, None, "tp"), P(seq, "tp"), P(seq, "tp")),
        check_vma=False,
    )
```

```python
import math

import jax
import jax.numpy as jnp
import numpy as np
from jax import lax
from jax.experimental import pallas as pl
from jax.experimental.pallas import tpu as pltpu
from jax.sharding import Mesh
from jax.sharding import PartitionSpec as P

HD = 128
TREE = 32
A_MAX = 8
GROUP = 4


NEG = -1e30


def ancestry(parents):
    length = parents.shape[-1]
    members = jnp.arange(length, dtype=jnp.int32)
    step = (members[:, None] == members[None, :]) | (parents[:, None] == members[None, :])
    reach = step.astype(jnp.bfloat16)
    covered = 1
    while covered < length - 1:
        reach = (
            jnp.dot(reach, reach, preferred_element_type=jnp.float32) > 0
        ).astype(jnp.bfloat16)
        covered *= 2
    return reach > 0


def load_kernel(weight_hbm, weight_vmem, done):
    copy = pltpu.make_async_copy(weight_hbm, weight_vmem, done)
    copy.start()
    copy.wait()


def load_weight(weight):
    return pl.pallas_call(
        load_kernel,
        in_specs=[pl.BlockSpec(memory_space=pl.ANY)],
        out_specs=pl.BlockSpec(memory_space=pltpu.VMEM),
        out_shape=jax.ShapeDtypeStruct(weight.shape, weight.dtype),
        scratch_shapes=[pltpu.SemaphoreType.DMA(())],
    )(weight)


def project_kernel(attention_ref, weight_ref, out_ref):
    result = jnp.dot(attention_ref[...], weight_ref[...], preferred_element_type=jnp.float32)
    width = out_ref.shape[2]
    for piece in range(out_ref.shape[0]):
        out_ref[piece] = result[:, piece * width : (piece + 1) * width].astype(out_ref.dtype)


def project(attention, weight, pieces):
    width = weight.shape[1] // pieces
    return pl.pallas_call(
        project_kernel,
        in_specs=[
            pl.BlockSpec(memory_space=pltpu.VMEM),
            pl.BlockSpec(memory_space=pltpu.VMEM),
        ],
        out_specs=pl.BlockSpec(memory_space=pltpu.VMEM),
        out_shape=jax.ShapeDtypeStruct((pieces, attention.shape[0], width), jnp.bfloat16),
    )(attention, weight)


def scale_heads(values, factors):
    return (values.reshape(factors.shape + (HD,)) * factors[..., None]).reshape(values.shape)


def on_device(
    queries,
    tree_keys,
    tree_values,
    cache_keys,
    cache_values,
    residual,
    out_weight,
    cache_len,
    parents,
    accept_rows,
    accept_len,
):
    member = lax.axis_index("mem")
    seq_rank = lax.axis_index("grp") * GROUP + member
    positions = cache_keys.shape[0]
    channels = cache_keys.shape[1]
    kv_local = channels // HD
    q_width = queries.shape[2]
    heads_local = q_width // HD
    sharing = heads_local // kv_local
    factor = 1.0 / math.sqrt(HD)
    regions = cache_len + A_MAX
    starts = jnp.cumsum(regions) - regions
    low_edge = seq_rank * positions
    places = low_edge + jnp.arange(positions, dtype=jnp.int32)
    keys_local = cache_keys.reshape(positions, kv_local, HD)
    values_local = cache_values.reshape(positions, kv_local, HD)

    sent = jnp.broadcast_to(queries, (GROUP,) + queries.shape[1:])
    gathered_q = lax.all_to_all(sent, "mem", 0, 0, tiled=True)

    group_base = seq_rank - member
    begin = lax.dynamic_slice_in_dim(starts, group_base, GROUP)
    length = lax.dynamic_slice_in_dim(cache_len, group_base, GROUP)
    inside = (places[None, :] >= begin[:, None]) & (places[None, :] < (begin + length)[:, None])
    shaped = gathered_q.reshape(GROUP, TREE, kv_local, sharing, HD)
    scores = (
        jnp.einsum("rtkgd,pkd->rkgtp", shaped, keys_local, preferred_element_type=jnp.float32)
        * factor
    )
    valid = inside[:, None, None, None, :]
    top_score = jnp.max(jnp.where(valid, scores, NEG), axis=-1)
    raised = jnp.where(valid, jnp.exp(scores - top_score[..., None]), 0.0)
    total = jnp.sum(raised, axis=-1)
    summed = jnp.einsum(
        "rkgtp,pkd->rtkgd",
        raised.astype(jnp.bfloat16),
        values_local,
        preferred_element_type=jnp.float32,
    )
    stats = jnp.concatenate(
        [top_score.reshape(GROUP, 1, -1), total.reshape(GROUP, 1, -1)], axis=-1
    )
    stats = jnp.pad(stats, ((0, 0), (0, 0), (0, q_width - stats.shape[-1])))
    tree_pair = jnp.concatenate([tree_keys[0], tree_values[0]], axis=-1)
    mine_rows = jnp.take(tree_pair, accept_rows[0], axis=0).astype(jnp.float32)
    row_lines = mine_rows.reshape(1, -1, q_width)
    row_count = row_lines.shape[1]
    row_lines = jnp.broadcast_to(row_lines, (GROUP,) + row_lines.shape[1:])
    used = TREE + 1 + row_count
    filler = jnp.zeros((GROUP, -used % 8, q_width), jnp.float32)
    message = jnp.concatenate(
        [summed.reshape(GROUP, TREE, q_width), stats, row_lines, filler], axis=1
    )
    partials = lax.all_to_all(message, "mem", 0, 0, tiled=True)
    row_block = partials[:, TREE + 1 : used].reshape(GROUP, A_MAX, 2 * channels)
    row_block = row_block.astype(jnp.bfloat16)
    part_out = partials[:, :TREE]
    stat_count = kv_local * sharing * TREE
    part_stats = partials[:, TREE, : 2 * stat_count].reshape(GROUP, 2, heads_local, TREE)
    part_top = jnp.transpose(part_stats[:, 0], (0, 2, 1))
    part_total = jnp.transpose(part_stats[:, 1], (0, 2, 1))

    linked = ancestry(parents[0])
    shaped_q = queries[0].reshape(TREE, kv_local, sharing, HD)
    own_keys = tree_keys[0].reshape(TREE, kv_local, HD)
    own_values = tree_values[0].reshape(TREE, kv_local, HD)
    drafted = (
        jnp.einsum("tkgd,jkd->kgtj", shaped_q, own_keys, preferred_element_type=jnp.float32)
        * factor
    )
    tree_top = jnp.max(jnp.where(linked, drafted, NEG), axis=-1)
    tree_raised = jnp.where(linked, jnp.exp(drafted - tree_top[..., None]), 0.0)
    tree_total = jnp.sum(tree_raised, axis=-1)
    tree_out = jnp.einsum(
        "kgtj,jkd->tkgd",
        tree_raised.astype(jnp.bfloat16),
        own_values,
        preferred_element_type=jnp.float32,
    ).reshape(TREE, q_width)
    tree_top = jnp.transpose(tree_top, (2, 0, 1)).reshape(TREE, heads_local)
    tree_total = jnp.transpose(tree_total, (2, 0, 1)).reshape(TREE, heads_local)

    joint_top = jnp.maximum(jnp.max(part_top, axis=0), tree_top)
    part_factor = jnp.exp(part_top - joint_top[None])
    tree_factor = jnp.exp(tree_top - joint_top)
    joint_out = jnp.sum(scale_heads(part_out, part_factor), axis=0) + scale_heads(
        tree_out, tree_factor
    )
    joint_total = jnp.sum(part_total * part_factor, axis=0) + tree_total * tree_factor
    attention = scale_heads(joint_out, 1.0 / joint_total).astype(jnp.bfloat16)

    tp_size = lax.axis_size("tp")
    pieces = project(attention, load_weight(out_weight), tp_size)
    pieces = lax.all_to_all(pieces, "tp", 0, 0, tiled=True)
    summed_heads = jnp.sum(pieces.astype(jnp.float32), axis=0)
    mixed = (residual[0].astype(jnp.float32) + summed_heads).astype(jnp.bfloat16)[None]

    row_accepted = lax.dynamic_slice_in_dim(accept_len, group_base, GROUP)
    column = jnp.arange(A_MAX, dtype=jnp.int32)
    targets = begin[:, None] + length[:, None] + column[None, :] - low_edge
    keep_row = (column[None, :] < row_accepted[:, None]) & (targets >= 0) & (targets < positions)
    targets = jnp.where(keep_row, targets, positions).reshape(-1)
    rows = row_block.reshape(-1, 2 * channels)
    new_keys = cache_keys.at[targets].set(rows[:, :channels], mode="drop")
    new_values = cache_values.at[targets].set(rows[:, channels:], mode="drop")
    return (mixed, new_keys, new_values)


def solution(mesh):
    seq_size = mesh.shape["seq"]
    tp_size = mesh.shape["tp"]
    devices = np.asarray(mesh.devices).reshape(seq_size // GROUP, GROUP, tp_size)
    inner = Mesh(devices, ("grp", "mem", "tp"))
    seq = ("grp", "mem")
    return jax.shard_map(
        on_device,
        mesh=inner,
        in_specs=(
            P(seq, None, "tp"),
            P(seq, None, "tp"),
            P(seq, None, "tp"),
            P(seq, "tp"),
            P(seq, "tp"),
            P(seq, None, "tp"),
            P("tp", None),
            P(),
            P(seq, None),
            P(seq, None),
            P(),
        ),
        out_specs=(P(seq, None, "tp"), P(seq, "tp"), P(seq, "tp")),
        check_vma=False,
    )
```

```python
import math

import jax
import jax.numpy as jnp
import numpy as np
from jax import lax
from jax.experimental import pallas as pl
from jax.experimental.pallas import tpu as pltpu
from jax.sharding import Mesh
from jax.sharding import PartitionSpec as P

HD = 128
TREE = 32
A_MAX = 8
GROUP = 4


NEG = -1e30


def ancestry(parents):
    length = parents.shape[-1]
    members = jnp.arange(length, dtype=jnp.int32)
    step = (members[:, None] == members[None, :]) | (parents[:, None] == members[None, :])
    reach = step.astype(jnp.bfloat16)
    covered = 1
    while covered < length - 1:
        reach = (
            jnp.dot(reach, reach, preferred_element_type=jnp.float32) > 0
        ).astype(jnp.bfloat16)
        covered *= 2
    return reach > 0


CHUNKS = 8


def project_kernel(attention_ref, weight_hbm, out_ref, weight_vmem, landed):
    rows = weight_vmem.shape[1]
    copies = [
        pltpu.make_async_copy(
            weight_hbm.at[pl.ds(chunk * rows, rows)], weight_vmem.at[chunk], landed.at[chunk]
        )
        for chunk in range(CHUNKS)
    ]
    for copy in copies:
        copy.start()
    attention = attention_ref[...]
    result = None
    for chunk in range(CHUNKS):
        copies[chunk].wait()
        part = jnp.dot(
            attention[:, chunk * rows : (chunk + 1) * rows],
            weight_vmem[chunk],
            preferred_element_type=jnp.float32,
        )
        result = part if result is None else result + part
    width = out_ref.shape[2]
    for piece in range(out_ref.shape[0]):
        out_ref[piece] = result[:, piece * width : (piece + 1) * width].astype(out_ref.dtype)


def project(attention, weight, pieces):
    rows, cols = weight.shape
    return pl.pallas_call(
        project_kernel,
        in_specs=[
            pl.BlockSpec(memory_space=pltpu.VMEM),
            pl.BlockSpec(memory_space=pl.ANY),
        ],
        out_specs=pl.BlockSpec(memory_space=pltpu.VMEM),
        out_shape=jax.ShapeDtypeStruct((pieces, attention.shape[0], cols // pieces), jnp.bfloat16),
        scratch_shapes=[
            pltpu.VMEM((CHUNKS, rows // CHUNKS, cols), weight.dtype),
            pltpu.SemaphoreType.DMA((CHUNKS,)),
        ],
    )(attention, weight)


def scale_heads(values, factors):
    return (values.reshape(factors.shape + (HD,)) * factors[..., None]).reshape(values.shape)


def on_device(
    queries,
    tree_keys,
    tree_values,
    cache_keys,
    cache_values,
    residual,
    out_weight,
    cache_len,
    parents,
    accept_rows,
    accept_len,
):
    member = lax.axis_index("mem")
    seq_rank = lax.axis_index("grp") * GROUP + member
    positions = cache_keys.shape[0]
    channels = cache_keys.shape[1]
    kv_local = channels // HD
    q_width = queries.shape[2]
    heads_local = q_width // HD
    sharing = heads_local // kv_local
    factor = 1.0 / math.sqrt(HD)
    regions = cache_len + A_MAX
    starts = jnp.cumsum(regions) - regions
    low_edge = seq_rank * positions
    places = low_edge + jnp.arange(positions, dtype=jnp.int32)
    keys_local = cache_keys.reshape(positions, kv_local, HD)
    values_local = cache_values.reshape(positions, kv_local, HD)

    sent = jnp.broadcast_to(queries, (GROUP,) + queries.shape[1:])
    gathered_q = lax.all_to_all(sent, "mem", 0, 0, tiled=True)

    group_base = seq_rank - member
    begin = lax.dynamic_slice_in_dim(starts, group_base, GROUP)
    length = lax.dynamic_slice_in_dim(cache_len, group_base, GROUP)
    inside = (places[None, :] >= begin[:, None]) & (places[None, :] < (begin + length)[:, None])
    shaped = gathered_q.reshape(GROUP, TREE, kv_local, sharing, HD)
    scores = (
        jnp.einsum("rtkgd,pkd->rkgtp", shaped, keys_local, preferred_element_type=jnp.float32)
        * factor
    )
    valid = inside[:, None, None, None, :]
    top_score = jnp.max(jnp.where(valid, scores, NEG), axis=-1)
    raised = jnp.where(valid, jnp.exp(scores - top_score[..., None]), 0.0)
    total = jnp.sum(raised, axis=-1)
    summed = jnp.einsum(
        "rkgtp,pkd->rtkgd",
        raised.astype(jnp.bfloat16),
        values_local,
        preferred_element_type=jnp.float32,
    )
    stats = jnp.concatenate(
        [top_score.reshape(GROUP, 1, -1), total.reshape(GROUP, 1, -1)], axis=-1
    )
    stats = jnp.pad(stats, ((0, 0), (0, 0), (0, q_width - stats.shape[-1])))
    tree_pair = jnp.concatenate([tree_keys[0], tree_values[0]], axis=-1)
    mine_rows = jnp.take(tree_pair, accept_rows[0], axis=0).astype(jnp.float32)
    row_lines = mine_rows.reshape(1, -1, q_width)
    row_count = row_lines.shape[1]
    row_lines = jnp.broadcast_to(row_lines, (GROUP,) + row_lines.shape[1:])
    used = TREE + 1 + row_count
    filler = jnp.zeros((GROUP, -used % 8, q_width), jnp.float32)
    message = jnp.concatenate(
        [summed.reshape(GROUP, TREE, q_width), stats, row_lines, filler], axis=1
    )
    partials = lax.all_to_all(message, "mem", 0, 0, tiled=True)
    row_block = partials[:, TREE + 1 : used].reshape(GROUP, A_MAX, 2 * channels)
    row_block = row_block.astype(jnp.bfloat16)
    part_out = partials[:, :TREE]
    stat_count = kv_local * sharing * TREE
    part_stats = partials[:, TREE, : 2 * stat_count].reshape(GROUP, 2, heads_local, TREE)
    part_top = jnp.transpose(part_stats[:, 0], (0, 2, 1))
    part_total = jnp.transpose(part_stats[:, 1], (0, 2, 1))

    linked = ancestry(parents[0])
    shaped_q = queries[0].reshape(TREE, kv_local, sharing, HD)
    own_keys = tree_keys[0].reshape(TREE, kv_local, HD)
    own_values = tree_values[0].reshape(TREE, kv_local, HD)
    drafted = (
        jnp.einsum("tkgd,jkd->kgtj", shaped_q, own_keys, preferred_element_type=jnp.float32)
        * factor
    )
    tree_top = jnp.max(jnp.where(linked, drafted, NEG), axis=-1)
    tree_raised = jnp.where(linked, jnp.exp(drafted - tree_top[..., None]), 0.0)
    tree_total = jnp.sum(tree_raised, axis=-1)
    tree_out = jnp.einsum(
        "kgtj,jkd->tkgd",
        tree_raised.astype(jnp.bfloat16),
        own_values,
        preferred_element_type=jnp.float32,
    ).reshape(TREE, q_width)
    tree_top = jnp.transpose(tree_top, (2, 0, 1)).reshape(TREE, heads_local)
    tree_total = jnp.transpose(tree_total, (2, 0, 1)).reshape(TREE, heads_local)

    joint_top = jnp.maximum(jnp.max(part_top, axis=0), tree_top)
    part_factor = jnp.exp(part_top - joint_top[None])
    tree_factor = jnp.exp(tree_top - joint_top)
    joint_out = jnp.sum(scale_heads(part_out, part_factor), axis=0) + scale_heads(
        tree_out, tree_factor
    )
    joint_total = jnp.sum(part_total * part_factor, axis=0) + tree_total * tree_factor
    attention = scale_heads(joint_out, 1.0 / joint_total).astype(jnp.bfloat16)

    tp_size = lax.axis_size("tp")
    pieces = project(attention, out_weight, tp_size)
    pieces = lax.all_to_all(pieces, "tp", 0, 0, tiled=True)
    summed_heads = jnp.sum(pieces.astype(jnp.float32), axis=0)
    mixed = (residual[0].astype(jnp.float32) + summed_heads).astype(jnp.bfloat16)[None]

    row_accepted = lax.dynamic_slice_in_dim(accept_len, group_base, GROUP)
    column = jnp.arange(A_MAX, dtype=jnp.int32)
    targets = begin[:, None] + length[:, None] + column[None, :] - low_edge
    keep_row = (column[None, :] < row_accepted[:, None]) & (targets >= 0) & (targets < positions)
    targets = jnp.where(keep_row, targets, positions).reshape(-1)
    rows = row_block.reshape(-1, 2 * channels)
    new_keys = cache_keys.at[targets].set(rows[:, :channels], mode="drop")
    new_values = cache_values.at[targets].set(rows[:, channels:], mode="drop")
    return (mixed, new_keys, new_values)


def solution(mesh):
    seq_size = mesh.shape["seq"]
    tp_size = mesh.shape["tp"]
    devices = np.asarray(mesh.devices).reshape(seq_size // GROUP, GROUP, tp_size)
    inner = Mesh(devices, ("grp", "mem", "tp"))
    seq = ("grp", "mem")
    return jax.shard_map(
        on_device,
        mesh=inner,
        in_specs=(
            P(seq, None, "tp"),
            P(seq, None, "tp"),
            P(seq, None, "tp"),
            P(seq, "tp"),
            P(seq, "tp"),
            P(seq, None, "tp"),
            P("tp", None),
            P(),
            P(seq, None),
            P(seq, None),
            P(),
        ),
        out_specs=(P(seq, None, "tp"), P(seq, "tp"), P(seq, "tp")),
        check_vma=False,
    )
```

```python
import math

import jax
import jax.numpy as jnp
import numpy as np
from jax import lax
from jax.experimental import pallas as pl
from jax.experimental.pallas import tpu as pltpu
from jax.sharding import Mesh
from jax.sharding import PartitionSpec as P

HD = 128
TREE = 32
A_MAX = 8
GROUP = 4


NEG = -1e30


def ancestry(parents):
    length = parents.shape[-1]
    members = jnp.arange(length, dtype=jnp.int32)
    step = (members[:, None] == members[None, :]) | (parents[:, None] == members[None, :])
    reach = step.astype(jnp.bfloat16)
    covered = 1
    while covered < length - 1:
        reach = (
            jnp.dot(reach, reach, preferred_element_type=jnp.float32) > 0
        ).astype(jnp.bfloat16)
        covered *= 2
    return reach > 0


def copies_kernel(source_hbm, target_hbm, landed):
    copies = [
        pltpu.make_async_copy(source_hbm, target_hbm.at[pl.ds(slot, 1)], landed.at[slot])
        for slot in range(target_hbm.shape[0])
    ]
    for copy in copies:
        copy.start()
    for copy in copies:
        copy.wait()


def replicate(block, count):
    return pl.pallas_call(
        copies_kernel,
        in_specs=[pl.BlockSpec(memory_space=pl.ANY)],
        out_specs=pl.BlockSpec(memory_space=pl.ANY),
        out_shape=jax.ShapeDtypeStruct((count,) + block.shape[1:], block.dtype),
        scratch_shapes=[pltpu.SemaphoreType.DMA((count,))],
    )(block)


def scale_heads(values, factors):
    return (values.reshape(factors.shape + (HD,)) * factors[..., None]).reshape(values.shape)


def on_device(
    queries,
    tree_keys,
    tree_values,
    cache_keys,
    cache_values,
    residual,
    out_weight,
    cache_len,
    parents,
    accept_rows,
    accept_len,
):
    member = lax.axis_index("mem")
    seq_rank = lax.axis_index("grp") * GROUP + member
    positions = cache_keys.shape[0]
    channels = cache_keys.shape[1]
    kv_local = channels // HD
    q_width = queries.shape[2]
    heads_local = q_width // HD
    sharing = heads_local // kv_local
    factor = 1.0 / math.sqrt(HD)
    regions = cache_len + A_MAX
    starts = jnp.cumsum(regions) - regions
    low_edge = seq_rank * positions
    places = low_edge + jnp.arange(positions, dtype=jnp.int32)
    keys_local = cache_keys.reshape(positions, kv_local, HD)
    values_local = cache_values.reshape(positions, kv_local, HD)

    sent = replicate(queries, GROUP)
    gathered_q = lax.all_to_all(sent, "mem", 0, 0, tiled=True)

    group_base = seq_rank - member
    begin = lax.dynamic_slice_in_dim(starts, group_base, GROUP)
    length = lax.dynamic_slice_in_dim(cache_len, group_base, GROUP)
    inside = (places[None, :] >= begin[:, None]) & (places[None, :] < (begin + length)[:, None])
    shaped = gathered_q.reshape(GROUP, TREE, kv_local, sharing, HD)
    scores = (
        jnp.einsum("rtkgd,pkd->rkgtp", shaped, keys_local, preferred_element_type=jnp.float32)
        * factor
    )
    valid = inside[:, None, None, None, :]
    top_score = jnp.max(jnp.where(valid, scores, NEG), axis=-1)
    raised = jnp.where(valid, jnp.exp(scores - top_score[..., None]), 0.0)
    total = jnp.sum(raised, axis=-1)
    summed = jnp.einsum(
        "rkgtp,pkd->rtkgd",
        raised.astype(jnp.bfloat16),
        values_local,
        preferred_element_type=jnp.float32,
    )
    stats = jnp.concatenate(
        [top_score.reshape(GROUP, 1, -1), total.reshape(GROUP, 1, -1)], axis=-1
    )
    stats = jnp.pad(stats, ((0, 0), (0, 0), (0, q_width - stats.shape[-1])))
    tree_pair = jnp.concatenate([tree_keys[0], tree_values[0]], axis=-1)
    mine_rows = jnp.take(tree_pair, accept_rows[0], axis=0).astype(jnp.float32)
    row_lines = mine_rows.reshape(1, -1, q_width)
    row_count = row_lines.shape[1]
    row_lines = jnp.broadcast_to(row_lines, (GROUP,) + row_lines.shape[1:])
    used = TREE + 1 + row_count
    filler = jnp.zeros((GROUP, -used % 8, q_width), jnp.float32)
    message = jnp.concatenate(
        [summed.reshape(GROUP, TREE, q_width), stats, row_lines, filler], axis=1
    )
    partials = lax.all_to_all(message, "mem", 0, 0, tiled=True)
    row_block = partials[:, TREE + 1 : used].reshape(GROUP, A_MAX, 2 * channels)
    row_block = row_block.astype(jnp.bfloat16)
    part_out = partials[:, :TREE]
    stat_count = kv_local * sharing * TREE
    part_stats = partials[:, TREE, : 2 * stat_count].reshape(GROUP, 2, heads_local, TREE)
    part_top = jnp.transpose(part_stats[:, 0], (0, 2, 1))
    part_total = jnp.transpose(part_stats[:, 1], (0, 2, 1))

    linked = ancestry(parents[0])
    shaped_q = queries[0].reshape(TREE, kv_local, sharing, HD)
    own_keys = tree_keys[0].reshape(TREE, kv_local, HD)
    own_values = tree_values[0].reshape(TREE, kv_local, HD)
    drafted = (
        jnp.einsum("tkgd,jkd->kgtj", shaped_q, own_keys, preferred_element_type=jnp.float32)
        * factor
    )
    tree_top = jnp.max(jnp.where(linked, drafted, NEG), axis=-1)
    tree_raised = jnp.where(linked, jnp.exp(drafted - tree_top[..., None]), 0.0)
    tree_total = jnp.sum(tree_raised, axis=-1)
    tree_out = jnp.einsum(
        "kgtj,jkd->tkgd",
        tree_raised.astype(jnp.bfloat16),
        own_values,
        preferred_element_type=jnp.float32,
    ).reshape(TREE, q_width)
    tree_top = jnp.transpose(tree_top, (2, 0, 1)).reshape(TREE, heads_local)
    tree_total = jnp.transpose(tree_total, (2, 0, 1)).reshape(TREE, heads_local)

    joint_top = jnp.maximum(jnp.max(part_top, axis=0), tree_top)
    part_factor = jnp.exp(part_top - joint_top[None])
    tree_factor = jnp.exp(tree_top - joint_top)
    joint_out = jnp.sum(scale_heads(part_out, part_factor), axis=0) + scale_heads(
        tree_out, tree_factor
    )
    joint_total = jnp.sum(part_total * part_factor, axis=0) + tree_total * tree_factor
    attention = scale_heads(joint_out, 1.0 / joint_total).astype(jnp.bfloat16)

    tp_size = lax.axis_size("tp")
    projected = lax.dot_general(
        out_weight, attention, (((0,), (1,)), ((), ())), preferred_element_type=jnp.float32
    ).astype(jnp.bfloat16)
    pieces = projected.reshape(tp_size, -1, TREE)
    pieces = lax.all_to_all(pieces, "tp", 0, 0, tiled=True)
    summed_heads = jnp.sum(pieces.astype(jnp.float32), axis=0)
    mixed = (residual[0].astype(jnp.float32) + summed_heads.T).astype(jnp.bfloat16)[None]

    row_accepted = lax.dynamic_slice_in_dim(accept_len, group_base, GROUP)
    column = jnp.arange(A_MAX, dtype=jnp.int32)
    targets = begin[:, None] + length[:, None] + column[None, :] - low_edge
    keep_row = (column[None, :] < row_accepted[:, None]) & (targets >= 0) & (targets < positions)
    targets = jnp.where(keep_row, targets, positions).reshape(-1)
    rows = row_block.reshape(-1, 2 * channels)
    new_keys = cache_keys.at[targets].set(rows[:, :channels], mode="drop")
    new_values = cache_values.at[targets].set(rows[:, channels:], mode="drop")
    return (mixed, new_keys, new_values)


def solution(mesh):
    seq_size = mesh.shape["seq"]
    tp_size = mesh.shape["tp"]
    devices = np.asarray(mesh.devices).reshape(seq_size // GROUP, GROUP, tp_size)
    inner = Mesh(devices, ("grp", "mem", "tp"))
    seq = ("grp", "mem")
    return jax.shard_map(
        on_device,
        mesh=inner,
        in_specs=(
            P(seq, None, "tp"),
            P(seq, None, "tp"),
            P(seq, None, "tp"),
            P(seq, "tp"),
            P(seq, "tp"),
            P(seq, None, "tp"),
            P("tp", None),
            P(),
            P(seq, None),
            P(seq, None),
            P(),
        ),
        out_specs=(P(seq, None, "tp"), P(seq, "tp"), P(seq, "tp")),
        check_vma=False,
    )
```

```python
import math

import jax
import jax.numpy as jnp
import numpy as np
from jax import lax
from jax.experimental import pallas as pl
from jax.experimental.pallas import tpu as pltpu
from jax.sharding import Mesh
from jax.sharding import PartitionSpec as P

HD = 128
TREE = 32
A_MAX = 8
GROUP = 4


NEG = -1e30


def ancestry(parents):
    length = parents.shape[-1]
    members = jnp.arange(length, dtype=jnp.int32)
    step = (members[:, None] == members[None, :]) | (parents[:, None] == members[None, :])
    reach = step.astype(jnp.bfloat16)
    covered = 1
    while covered < length - 1:
        reach = (
            jnp.dot(reach, reach, preferred_element_type=jnp.float32) > 0
        ).astype(jnp.bfloat16)
        covered *= 2
    return reach > 0


CHUNKS = 8


def project_kernel(attention_ref, weight_hbm, out_ref, weight_vmem, landed):
    rows = weight_vmem.shape[1]
    copies = [
        pltpu.make_async_copy(
            weight_hbm.at[pl.ds(chunk * rows, rows)], weight_vmem.at[chunk], landed.at[chunk]
        )
        for chunk in range(CHUNKS)
    ]
    for copy in copies:
        copy.start()
    attention = attention_ref[...]
    result = None
    for chunk in range(CHUNKS):
        copies[chunk].wait()
        part = jnp.dot(
            attention[:, chunk * rows : (chunk + 1) * rows],
            weight_vmem[chunk],
            preferred_element_type=jnp.float32,
        )
        result = part if result is None else result + part
    width = out_ref.shape[2]
    for piece in range(out_ref.shape[0]):
        out_ref[piece] = result[:, piece * width : (piece + 1) * width].astype(out_ref.dtype)


def project(attention, weight, pieces):
    rows, cols = weight.shape
    return pl.pallas_call(
        project_kernel,
        in_specs=[
            pl.BlockSpec(memory_space=pltpu.VMEM),
            pl.BlockSpec(memory_space=pl.ANY),
        ],
        out_specs=pl.BlockSpec(memory_space=pltpu.VMEM),
        out_shape=jax.ShapeDtypeStruct((pieces, attention.shape[0], cols // pieces), jnp.bfloat16),
        scratch_shapes=[
            pltpu.VMEM((CHUNKS, rows // CHUNKS, cols), weight.dtype),
            pltpu.SemaphoreType.DMA((CHUNKS,)),
        ],
    )(attention, weight)


def scale_heads(values, factors):
    return (values.reshape(factors.shape + (HD,)) * factors[..., None]).reshape(values.shape)


def on_device(
    queries,
    tree_keys,
    tree_values,
    cache_keys,
    cache_values,
    residual,
    out_weight,
    cache_len,
    parents,
    accept_rows,
    accept_len,
):
    member = lax.axis_index("mem")
    seq_rank = lax.axis_index("grp") * GROUP + member
    positions = cache_keys.shape[0]
    channels = cache_keys.shape[1]
    kv_local = channels // HD
    q_width = queries.shape[2]
    heads_local = q_width // HD
    sharing = heads_local // kv_local
    factor = 1.0 / math.sqrt(HD)
    regions = cache_len + A_MAX
    starts = jnp.cumsum(regions) - regions
    low_edge = seq_rank * positions
    places = low_edge + jnp.arange(positions, dtype=jnp.int32)
    keys_local = cache_keys.reshape(positions, kv_local, HD)
    values_local = cache_values.reshape(positions, kv_local, HD)

    sent = jnp.broadcast_to(queries, (GROUP,) + queries.shape[1:])
    gathered_q = lax.all_to_all(sent, "mem", 0, 0, tiled=True)

    group_base = seq_rank - member
    begin = lax.dynamic_slice_in_dim(starts, group_base, GROUP)
    length = lax.dynamic_slice_in_dim(cache_len, group_base, GROUP)
    inside = (places[None, :] >= begin[:, None]) & (places[None, :] < (begin + length)[:, None])
    shaped = gathered_q.reshape(GROUP, TREE, kv_local, sharing, HD)
    scores = (
        jnp.einsum("rtkgd,pkd->rkgtp", shaped, keys_local, preferred_element_type=jnp.float32)
        * factor
    )
    valid = inside[:, None, None, None, :]
    top_score = jnp.max(jnp.where(valid, scores, NEG), axis=-1)
    top_score = top_score.astype(jnp.bfloat16).astype(jnp.float32)
    raised = jnp.where(valid, jnp.exp(scores - top_score[..., None]), 0.0)
    total = jnp.sum(raised, axis=-1)
    summed = jnp.einsum(
        "rkgtp,pkd->rtkgd",
        raised.astype(jnp.bfloat16),
        values_local,
        preferred_element_type=jnp.float32,
    )
    stats = jnp.concatenate(
        [top_score.reshape(GROUP, 1, -1), total.reshape(GROUP, 1, -1)], axis=-1
    ).astype(jnp.bfloat16)
    stats = jnp.pad(stats, ((0, 0), (0, 0), (0, q_width - stats.shape[-1])))
    tree_pair = jnp.concatenate([tree_keys[0], tree_values[0]], axis=-1)
    mine_rows = jnp.take(tree_pair, accept_rows[0], axis=0)
    row_lines = mine_rows.reshape(1, -1, q_width)
    row_count = row_lines.shape[1]
    row_lines = jnp.broadcast_to(row_lines, (GROUP,) + row_lines.shape[1:])
    used = TREE + 1 + row_count
    filler = jnp.zeros((GROUP, -used % 16, q_width), jnp.bfloat16)
    message = jnp.concatenate(
        [summed.reshape(GROUP, TREE, q_width).astype(jnp.bfloat16), stats, row_lines, filler],
        axis=1,
    )
    message, queries, tree_keys, tree_values, parents = lax.optimization_barrier(
        (message, queries, tree_keys, tree_values, parents)
    )
    partials = lax.all_to_all(message, "mem", 0, 0, tiled=True)
    row_block = partials[:, TREE + 1 : used].reshape(GROUP, A_MAX, 2 * channels)
    partials = partials.astype(jnp.float32)
    part_out = partials[:, :TREE]
    stat_count = kv_local * sharing * TREE
    part_stats = partials[:, TREE, : 2 * stat_count].reshape(GROUP, 2, heads_local, TREE)
    part_top = jnp.transpose(part_stats[:, 0], (0, 2, 1))
    part_total = jnp.transpose(part_stats[:, 1], (0, 2, 1))

    linked = ancestry(parents[0])
    shaped_q = queries[0].reshape(TREE, kv_local, sharing, HD)
    own_keys = tree_keys[0].reshape(TREE, kv_local, HD)
    own_values = tree_values[0].reshape(TREE, kv_local, HD)
    drafted = (
        jnp.einsum("tkgd,jkd->kgtj", shaped_q, own_keys, preferred_element_type=jnp.float32)
        * factor
    )
    tree_top = jnp.max(jnp.where(linked, drafted, NEG), axis=-1)
    tree_raised = jnp.where(linked, jnp.exp(drafted - tree_top[..., None]), 0.0)
    tree_total = jnp.sum(tree_raised, axis=-1)
    tree_out = jnp.einsum(
        "kgtj,jkd->tkgd",
        tree_raised.astype(jnp.bfloat16),
        own_values,
        preferred_element_type=jnp.float32,
    ).reshape(TREE, q_width)
    tree_top = jnp.transpose(tree_top, (2, 0, 1)).reshape(TREE, heads_local)
    tree_total = jnp.transpose(tree_total, (2, 0, 1)).reshape(TREE, heads_local)

    joint_top = jnp.maximum(jnp.max(part_top, axis=0), tree_top)
    part_factor = jnp.exp(part_top - joint_top[None])
    tree_factor = jnp.exp(tree_top - joint_top)
    joint_out = jnp.sum(scale_heads(part_out, part_factor), axis=0) + scale_heads(
        tree_out, tree_factor
    )
    joint_total = jnp.sum(part_total * part_factor, axis=0) + tree_total * tree_factor
    attention = scale_heads(joint_out, 1.0 / joint_total).astype(jnp.bfloat16)

    tp_size = lax.axis_size("tp")
    pieces = project(attention, out_weight, tp_size)
    pieces = lax.all_to_all(pieces, "tp", 0, 0, tiled=True)
    summed_heads = jnp.sum(pieces.astype(jnp.float32), axis=0)
    mixed = (residual[0].astype(jnp.float32) + summed_heads).astype(jnp.bfloat16)[None]

    row_accepted = lax.dynamic_slice_in_dim(accept_len, group_base, GROUP)
    column = jnp.arange(A_MAX, dtype=jnp.int32)
    targets = begin[:, None] + length[:, None] + column[None, :] - low_edge
    keep_row = (column[None, :] < row_accepted[:, None]) & (targets >= 0) & (targets < positions)
    targets = jnp.where(keep_row, targets, positions).reshape(-1)
    rows = row_block.reshape(-1, 2 * channels)
    new_keys = cache_keys.at[targets].set(rows[:, :channels], mode="drop")
    new_values = cache_values.at[targets].set(rows[:, channels:], mode="drop")
    return (mixed, new_keys, new_values)


def solution(mesh):
    seq_size = mesh.shape["seq"]
    tp_size = mesh.shape["tp"]
    devices = np.asarray(mesh.devices).reshape(seq_size // GROUP, GROUP, tp_size)
    inner = Mesh(devices, ("grp", "mem", "tp"))
    seq = ("grp", "mem")
    return jax.shard_map(
        on_device,
        mesh=inner,
        in_specs=(
            P(seq, None, "tp"),
            P(seq, None, "tp"),
            P(seq, None, "tp"),
            P(seq, "tp"),
            P(seq, "tp"),
            P(seq, None, "tp"),
            P("tp", None),
            P(),
            P(seq, None),
            P(seq, None),
            P(),
        ),
        out_specs=(P(seq, None, "tp"), P(seq, "tp"), P(seq, "tp")),
        check_vma=False,
    )
```

```python
import math

import jax
import jax.numpy as jnp
import numpy as np
from jax import lax
from jax.experimental import pallas as pl
from jax.experimental.pallas import tpu as pltpu
from jax.sharding import Mesh
from jax.sharding import PartitionSpec as P

HD = 128
TREE = 32
A_MAX = 8
GROUP = 4


NEG = -1e30


def ancestry(parents):
    length = parents.shape[-1]
    members = jnp.arange(length, dtype=jnp.int32)
    step = (members[:, None] == members[None, :]) | (parents[:, None] == members[None, :])
    reach = step.astype(jnp.bfloat16)
    covered = 1
    while covered < length - 1:
        reach = (
            jnp.dot(reach, reach, preferred_element_type=jnp.float32) > 0
        ).astype(jnp.bfloat16)
        covered *= 2
    return reach > 0


CHUNKS = 8


def project_kernel(attention_ref, weight_hbm, out_ref, weight_vmem, landed):
    rows = weight_vmem.shape[1]
    copies = [
        pltpu.make_async_copy(
            weight_hbm.at[pl.ds(chunk * rows, rows)], weight_vmem.at[chunk], landed.at[chunk]
        )
        for chunk in range(CHUNKS)
    ]
    for copy in copies:
        copy.start()
    attention = attention_ref[...]
    result = None
    for chunk in range(CHUNKS):
        copies[chunk].wait()
        part = jnp.dot(
            attention[:, chunk * rows : (chunk + 1) * rows],
            weight_vmem[chunk],
            preferred_element_type=jnp.float32,
        )
        result = part if result is None else result + part
    width = out_ref.shape[2]
    for piece in range(out_ref.shape[0]):
        out_ref[piece] = result[:, piece * width : (piece + 1) * width].astype(out_ref.dtype)


def project(attention, weight, pieces):
    rows, cols = weight.shape
    return pl.pallas_call(
        project_kernel,
        in_specs=[
            pl.BlockSpec(memory_space=pltpu.VMEM),
            pl.BlockSpec(memory_space=pl.ANY),
        ],
        out_specs=pl.BlockSpec(memory_space=pltpu.VMEM),
        out_shape=jax.ShapeDtypeStruct((pieces, attention.shape[0], cols // pieces), jnp.bfloat16),
        scratch_shapes=[
            pltpu.VMEM((CHUNKS, rows // CHUNKS, cols), weight.dtype),
            pltpu.SemaphoreType.DMA((CHUNKS,)),
        ],
    )(attention, weight)


def scale_heads(values, factors):
    return (values.reshape(factors.shape + (HD,)) * factors[..., None]).reshape(values.shape)


def on_device(
    queries,
    tree_keys,
    tree_values,
    cache_keys,
    cache_values,
    residual,
    out_weight,
    cache_len,
    parents,
    accept_rows,
    accept_len,
):
    member = lax.axis_index("mem")
    seq_rank = lax.axis_index("grp") * GROUP + member
    positions = cache_keys.shape[0]
    channels = cache_keys.shape[1]
    kv_local = channels // HD
    q_width = queries.shape[2]
    heads_local = q_width // HD
    sharing = heads_local // kv_local
    factor = 1.0 / math.sqrt(HD)
    regions = cache_len + A_MAX
    starts = jnp.cumsum(regions) - regions
    low_edge = seq_rank * positions
    places = low_edge + jnp.arange(positions, dtype=jnp.int32)

    sent = jnp.broadcast_to(queries, (GROUP,) + queries.shape[1:])
    sent, cache_keys, cache_values = lax.optimization_barrier((sent, cache_keys, cache_values))
    keys_local = cache_keys.reshape(positions, kv_local, HD)
    values_local = cache_values.reshape(positions, kv_local, HD)
    gathered_q = lax.all_to_all(sent, "mem", 0, 0, tiled=True)

    group_base = seq_rank - member
    begin = lax.dynamic_slice_in_dim(starts, group_base, GROUP)
    length = lax.dynamic_slice_in_dim(cache_len, group_base, GROUP)
    inside = (places[None, :] >= begin[:, None]) & (places[None, :] < (begin + length)[:, None])
    shaped = gathered_q.reshape(GROUP, TREE, kv_local, sharing, HD)
    scores = (
        jnp.einsum("rtkgd,pkd->rkgtp", shaped, keys_local, preferred_element_type=jnp.float32)
        * factor
    )
    valid = inside[:, None, None, None, :]
    top_score = jnp.max(jnp.where(valid, scores, NEG), axis=-1)
    top_score = top_score.astype(jnp.bfloat16).astype(jnp.float32)
    raised = jnp.where(valid, jnp.exp(scores - top_score[..., None]), 0.0)
    total = jnp.sum(raised, axis=-1)
    summed = jnp.einsum(
        "rkgtp,pkd->rtkgd",
        raised.astype(jnp.bfloat16),
        values_local,
        preferred_element_type=jnp.float32,
    )
    stats = jnp.concatenate(
        [top_score.reshape(GROUP, 1, -1), total.reshape(GROUP, 1, -1)], axis=-1
    ).astype(jnp.bfloat16)
    stats = jnp.pad(stats, ((0, 0), (0, 0), (0, q_width - stats.shape[-1])))
    tree_pair = jnp.concatenate([tree_keys[0], tree_values[0]], axis=-1)
    mine_rows = jnp.take(tree_pair, accept_rows[0], axis=0)
    row_lines = mine_rows.reshape(1, -1, q_width)
    row_count = row_lines.shape[1]
    row_lines = jnp.broadcast_to(row_lines, (GROUP,) + row_lines.shape[1:])
    used = TREE + 1 + row_count
    filler = jnp.zeros((GROUP, -used % 16, q_width), jnp.bfloat16)
    message = jnp.concatenate(
        [summed.reshape(GROUP, TREE, q_width).astype(jnp.bfloat16), stats, row_lines, filler],
        axis=1,
    )
    message, queries, tree_keys, tree_values, parents = lax.optimization_barrier(
        (message, queries, tree_keys, tree_values, parents)
    )
    partials = lax.all_to_all(message, "mem", 0, 0, tiled=True)
    row_block = partials[:, TREE + 1 : used].reshape(GROUP, A_MAX, 2 * channels)
    partials = partials.astype(jnp.float32)
    part_out = partials[:, :TREE]
    stat_count = kv_local * sharing * TREE
    part_stats = partials[:, TREE, : 2 * stat_count].reshape(GROUP, 2, heads_local, TREE)
    part_top = jnp.transpose(part_stats[:, 0], (0, 2, 1))
    part_total = jnp.transpose(part_stats[:, 1], (0, 2, 1))

    linked = ancestry(parents[0])
    shaped_q = queries[0].reshape(TREE, kv_local, sharing, HD)
    own_keys = tree_keys[0].reshape(TREE, kv_local, HD)
    own_values = tree_values[0].reshape(TREE, kv_local, HD)
    drafted = (
        jnp.einsum("tkgd,jkd->kgtj", shaped_q, own_keys, preferred_element_type=jnp.float32)
        * factor
    )
    tree_top = jnp.max(jnp.where(linked, drafted, NEG), axis=-1)
    tree_raised = jnp.where(linked, jnp.exp(drafted - tree_top[..., None]), 0.0)
    tree_total = jnp.sum(tree_raised, axis=-1)
    tree_out = jnp.einsum(
        "kgtj,jkd->tkgd",
        tree_raised.astype(jnp.bfloat16),
        own_values,
        preferred_element_type=jnp.float32,
    ).reshape(TREE, q_width)
    tree_top = jnp.transpose(tree_top, (2, 0, 1)).reshape(TREE, heads_local)
    tree_total = jnp.transpose(tree_total, (2, 0, 1)).reshape(TREE, heads_local)

    joint_top = jnp.maximum(jnp.max(part_top, axis=0), tree_top)
    part_factor = jnp.exp(part_top - joint_top[None])
    tree_factor = jnp.exp(tree_top - joint_top)
    joint_out = jnp.sum(scale_heads(part_out, part_factor), axis=0) + scale_heads(
        tree_out, tree_factor
    )
    joint_total = jnp.sum(part_total * part_factor, axis=0) + tree_total * tree_factor
    attention = scale_heads(joint_out, 1.0 / joint_total).astype(jnp.bfloat16)

    tp_size = lax.axis_size("tp")
    projected = lax.dot_general(
        out_weight, attention, (((0,), (1,)), ((), ())), preferred_element_type=jnp.float32
    ).astype(jnp.bfloat16)
    pieces = projected.reshape(tp_size, -1, TREE)
    pieces = lax.all_to_all(pieces, "tp", 0, 0, tiled=True)
    summed_heads = jnp.sum(pieces.astype(jnp.float32), axis=0)
    mixed = (residual[0].astype(jnp.float32) + summed_heads.T).astype(jnp.bfloat16)[None]

    row_accepted = lax.dynamic_slice_in_dim(accept_len, group_base, GROUP)
    column = jnp.arange(A_MAX, dtype=jnp.int32)
    targets = begin[:, None] + length[:, None] + column[None, :] - low_edge
    keep_row = (column[None, :] < row_accepted[:, None]) & (targets >= 0) & (targets < positions)
    targets = jnp.where(keep_row, targets, positions).reshape(-1)
    rows = row_block.reshape(-1, 2 * channels)
    new_keys = cache_keys.at[targets].set(rows[:, :channels], mode="drop")
    new_values = cache_values.at[targets].set(rows[:, channels:], mode="drop")
    return (mixed, new_keys, new_values)


def solution(mesh):
    seq_size = mesh.shape["seq"]
    tp_size = mesh.shape["tp"]
    devices = np.asarray(mesh.devices).reshape(seq_size // GROUP, GROUP, tp_size)
    inner = Mesh(devices, ("grp", "mem", "tp"))
    seq = ("grp", "mem")
    return jax.shard_map(
        on_device,
        mesh=inner,
        in_specs=(
            P(seq, None, "tp"),
            P(seq, None, "tp"),
            P(seq, None, "tp"),
            P(seq, "tp"),
            P(seq, "tp"),
            P(seq, None, "tp"),
            P("tp", None),
            P(),
            P(seq, None),
            P(seq, None),
            P(),
        ),
        out_specs=(P(seq, None, "tp"), P(seq, "tp"), P(seq, "tp")),
        check_vma=False,
    )
```

```python
import math

import jax
import jax.numpy as jnp
import numpy as np
from jax import lax
from jax.experimental import pallas as pl
from jax.experimental.pallas import tpu as pltpu
from jax.sharding import Mesh
from jax.sharding import PartitionSpec as P

HD = 128
TREE = 32
A_MAX = 8
GROUP = 4


NEG = -1e30


def ancestry(parents):
    length = parents.shape[-1]
    members = jnp.arange(length, dtype=jnp.int32)
    step = (members[:, None] == members[None, :]) | (parents[:, None] == members[None, :])
    reach = step.astype(jnp.bfloat16)
    covered = 1
    while covered < length - 1:
        reach = (
            jnp.dot(reach, reach, preferred_element_type=jnp.float32) > 0
        ).astype(jnp.bfloat16)
        covered *= 2
    return reach > 0


CHUNKS = 8


def project_kernel(attention_ref, weight_hbm, out_ref, weight_vmem, landed):
    rows = weight_vmem.shape[1]
    copies = [
        pltpu.make_async_copy(
            weight_hbm.at[pl.ds(chunk * rows, rows)], weight_vmem.at[chunk], landed.at[chunk]
        )
        for chunk in range(CHUNKS)
    ]
    for copy in copies:
        copy.start()
    attention = attention_ref[...]
    result = None
    for chunk in range(CHUNKS):
        copies[chunk].wait()
        part = jnp.dot(
            attention[:, chunk * rows : (chunk + 1) * rows],
            weight_vmem[chunk],
            preferred_element_type=jnp.float32,
        )
        result = part if result is None else result + part
    width = out_ref.shape[2]
    for piece in range(out_ref.shape[0]):
        out_ref[piece] = result[:, piece * width : (piece + 1) * width].astype(out_ref.dtype)


def project(attention, weight, pieces):
    rows, cols = weight.shape
    return pl.pallas_call(
        project_kernel,
        in_specs=[
            pl.BlockSpec(memory_space=pltpu.VMEM),
            pl.BlockSpec(memory_space=pl.ANY),
        ],
        out_specs=pl.BlockSpec(memory_space=pltpu.VMEM),
        out_shape=jax.ShapeDtypeStruct((pieces, attention.shape[0], cols // pieces), jnp.bfloat16),
        scratch_shapes=[
            pltpu.VMEM((CHUNKS, rows // CHUNKS, cols), weight.dtype),
            pltpu.SemaphoreType.DMA((CHUNKS,)),
        ],
    )(attention, weight)


def attend_kernel(
    bounds_ref, queries_ref, keys_hbm, values_hbm, extra_ref, out_ref, keys_vmem, values_vmem, landed
):
    keys_copy = pltpu.make_async_copy(keys_hbm, keys_vmem, landed.at[0])
    values_copy = pltpu.make_async_copy(values_hbm, values_vmem, landed.at[1])
    keys_copy.start()
    values_copy.start()
    count = out_ref.shape[0]
    tree = queries_ref.shape[1]
    heads = queries_ref.shape[2] // HD
    positions = keys_vmem.shape[0]
    factor = 1.0 / math.sqrt(HD)
    place = lax.broadcasted_iota(jnp.int32, (tree, positions), 1)
    lane = lax.broadcasted_iota(jnp.int32, (tree, HD), 1)
    pick = (
        lax.broadcasted_iota(jnp.int32, (16, HD), 0) == lax.broadcasted_iota(jnp.int32, (16, HD), 1)
    ) & (lax.broadcasted_iota(jnp.int32, (16, HD), 0) < 2 * heads)
    pick = pick.astype(jnp.bfloat16)
    spare = jnp.zeros((out_ref.shape[2] - tree, HD), jnp.bfloat16)
    keys_copy.wait()
    values_copy.wait()
    keys = keys_vmem[...]
    values = values_vmem[...]
    for request in range(count):
        valid = (place >= bounds_ref[request]) & (place < bounds_ref[count + request])
        stat = jnp.zeros((tree, HD), jnp.float32)
        for head in range(heads):
            rows = queries_ref[request, :, head * HD : (head + 1) * HD]
            scores = (
                lax.dot_general(
                    rows, keys, (((1,), (1,)), ((), ())), preferred_element_type=jnp.float32
                )
                * factor
            )
            top = jnp.max(jnp.where(valid, scores, NEG), axis=1, keepdims=True)
            top = top.astype(jnp.bfloat16).astype(jnp.float32)
            raised = jnp.where(valid, jnp.exp(scores - top), 0.0)
            total = jnp.sum(raised, axis=1, keepdims=True)
            summed = jnp.dot(
                raised.astype(jnp.bfloat16), values, preferred_element_type=jnp.float32
            )
            out_ref[request, 0:tree, head * HD : (head + 1) * HD] = summed.astype(out_ref.dtype)
            stat = jnp.where(lane == head, top, stat)
            total = total.astype(jnp.bfloat16).astype(jnp.float32)
            stat = jnp.where(lane == heads + head, total, stat)
        padded = jnp.concatenate([stat.astype(jnp.bfloat16), spare], axis=0)
        placed = lax.dot_general(
            pick, padded, (((1,), (1,)), ((), ())), preferred_element_type=jnp.float32
        )
        block = extra_ref[...].astype(jnp.float32) + placed
        out_ref[request, tree : tree + 16, :] = block.astype(out_ref.dtype)


def attend(bounds, queries, keys, values, extra):
    count, tree, width = queries.shape
    return pl.pallas_call(
        attend_kernel,
        in_specs=[
            pl.BlockSpec(memory_space=pltpu.SMEM),
            pl.BlockSpec(memory_space=pltpu.VMEM),
            pl.BlockSpec(memory_space=pl.ANY),
            pl.BlockSpec(memory_space=pl.ANY),
            pl.BlockSpec(memory_space=pltpu.VMEM),
        ],
        out_specs=pl.BlockSpec(memory_space=pltpu.VMEM),
        out_shape=jax.ShapeDtypeStruct((count, tree + 16, width), jnp.bfloat16),
        scratch_shapes=[
            pltpu.VMEM(keys.shape, keys.dtype),
            pltpu.VMEM(values.shape, values.dtype),
            pltpu.SemaphoreType.DMA((2,)),
        ],
    )(bounds, queries, keys, values, extra)


def scale_heads(values, factors):
    return (values.reshape(factors.shape + (HD,)) * factors[..., None]).reshape(values.shape)


def on_device(
    queries,
    tree_keys,
    tree_values,
    cache_keys,
    cache_values,
    residual,
    out_weight,
    cache_len,
    parents,
    accept_rows,
    accept_len,
):
    member = lax.axis_index("mem")
    seq_rank = lax.axis_index("grp") * GROUP + member
    positions = cache_keys.shape[0]
    channels = cache_keys.shape[1]
    kv_local = channels // HD
    q_width = queries.shape[2]
    heads_local = q_width // HD
    sharing = heads_local // kv_local
    factor = 1.0 / math.sqrt(HD)
    regions = cache_len + A_MAX
    starts = jnp.cumsum(regions) - regions
    low_edge = seq_rank * positions
    places = low_edge + jnp.arange(positions, dtype=jnp.int32)

    sent = jnp.broadcast_to(queries, (GROUP,) + queries.shape[1:])
    keys_local = cache_keys.reshape(positions, kv_local, HD)
    values_local = cache_values.reshape(positions, kv_local, HD)
    gathered_q = lax.all_to_all(sent, "mem", 0, 0, tiled=True)

    group_base = seq_rank - member
    begin = lax.dynamic_slice_in_dim(starts, group_base, GROUP)
    length = lax.dynamic_slice_in_dim(cache_len, group_base, GROUP)
    bounds = jnp.concatenate([begin - low_edge, begin + length - low_edge]).astype(jnp.int32)
    tree_pair = jnp.concatenate([tree_keys[0], tree_values[0]], axis=-1)
    mine_rows = jnp.take(tree_pair, accept_rows[0], axis=0)
    row_lines = mine_rows.reshape(-1, q_width)
    row_count = row_lines.shape[0]
    extra = jnp.zeros((16, q_width), jnp.bfloat16)
    extra = lax.dynamic_update_slice(extra, row_lines, (8, 0))
    message = attend(bounds, gathered_q, cache_keys, cache_values, extra)
    message, queries, tree_keys, tree_values, parents = lax.optimization_barrier(
        (message, queries, tree_keys, tree_values, parents)
    )
    partials = lax.all_to_all(message, "mem", 0, 0, tiled=True)
    row_block = partials[:, TREE + 8 : TREE + 8 + row_count].reshape(GROUP, A_MAX, 2 * channels)
    partials = partials.astype(jnp.float32)
    part_out = partials[:, :TREE]
    part_stats = partials[:, TREE : TREE + 2 * heads_local, :TREE]
    part_top = jnp.transpose(part_stats[:, :heads_local], (0, 2, 1))
    part_total = jnp.transpose(part_stats[:, heads_local:], (0, 2, 1))

    linked = ancestry(parents[0])
    shaped_q = queries[0].reshape(TREE, kv_local, sharing, HD)
    own_keys = tree_keys[0].reshape(TREE, kv_local, HD)
    own_values = tree_values[0].reshape(TREE, kv_local, HD)
    drafted = (
        jnp.einsum("tkgd,jkd->kgtj", shaped_q, own_keys, preferred_element_type=jnp.float32)
        * factor
    )
    tree_top = jnp.max(jnp.where(linked, drafted, NEG), axis=-1)
    tree_raised = jnp.where(linked, jnp.exp(drafted - tree_top[..., None]), 0.0)
    tree_total = jnp.sum(tree_raised, axis=-1)
    tree_out = jnp.einsum(
        "kgtj,jkd->tkgd",
        tree_raised.astype(jnp.bfloat16),
        own_values,
        preferred_element_type=jnp.float32,
    ).reshape(TREE, q_width)
    tree_top = jnp.transpose(tree_top, (2, 0, 1)).reshape(TREE, heads_local)
    tree_total = jnp.transpose(tree_total, (2, 0, 1)).reshape(TREE, heads_local)

    joint_top = jnp.maximum(jnp.max(part_top, axis=0), tree_top)
    part_factor = jnp.exp(part_top - joint_top[None])
    tree_factor = jnp.exp(tree_top - joint_top)
    joint_out = jnp.sum(scale_heads(part_out, part_factor), axis=0) + scale_heads(
        tree_out, tree_factor
    )
    joint_total = jnp.sum(part_total * part_factor, axis=0) + tree_total * tree_factor
    attention = scale_heads(joint_out, 1.0 / joint_total).astype(jnp.bfloat16)

    tp_size = lax.axis_size("tp")
    projected = lax.dot_general(
        out_weight, attention, (((0,), (1,)), ((), ())), preferred_element_type=jnp.float32
    ).astype(jnp.bfloat16)
    pieces = projected.reshape(tp_size, -1, TREE)
    pieces = lax.all_to_all(pieces, "tp", 0, 0, tiled=True)
    summed_heads = jnp.sum(pieces.astype(jnp.float32), axis=0)
    mixed = (residual[0].astype(jnp.float32) + summed_heads.T).astype(jnp.bfloat16)[None]

    row_accepted = lax.dynamic_slice_in_dim(accept_len, group_base, GROUP)
    column = jnp.arange(A_MAX, dtype=jnp.int32)
    targets = begin[:, None] + length[:, None] + column[None, :] - low_edge
    keep_row = (column[None, :] < row_accepted[:, None]) & (targets >= 0) & (targets < positions)
    targets = jnp.where(keep_row, targets, positions).reshape(-1)
    rows = row_block.reshape(-1, 2 * channels)
    new_keys = cache_keys.at[targets].set(rows[:, :channels], mode="drop")
    new_values = cache_values.at[targets].set(rows[:, channels:], mode="drop")
    return (mixed, new_keys, new_values)


def solution(mesh):
    seq_size = mesh.shape["seq"]
    tp_size = mesh.shape["tp"]
    devices = np.asarray(mesh.devices).reshape(seq_size // GROUP, GROUP, tp_size)
    inner = Mesh(devices, ("grp", "mem", "tp"))
    seq = ("grp", "mem")
    return jax.shard_map(
        on_device,
        mesh=inner,
        in_specs=(
            P(seq, None, "tp"),
            P(seq, None, "tp"),
            P(seq, None, "tp"),
            P(seq, "tp"),
            P(seq, "tp"),
            P(seq, None, "tp"),
            P("tp", None),
            P(),
            P(seq, None),
            P(seq, None),
            P(),
        ),
        out_specs=(P(seq, None, "tp"), P(seq, "tp"), P(seq, "tp")),
        check_vma=False,
    )
```

```python
import math

import jax
import jax.numpy as jnp
import numpy as np
from jax import lax
from jax.experimental import pallas as pl
from jax.experimental.pallas import tpu as pltpu
from jax.sharding import Mesh
from jax.sharding import PartitionSpec as P

HD = 128
TREE = 32
A_MAX = 8
GROUP = 4


NEG = -1e30


def ancestry(parents):
    length = parents.shape[-1]
    members = jnp.arange(length, dtype=jnp.int32)
    step = (members[:, None] == members[None, :]) | (parents[:, None] == members[None, :])
    reach = step.astype(jnp.bfloat16)
    covered = 1
    while covered < length - 1:
        reach = (
            jnp.dot(reach, reach, preferred_element_type=jnp.float32) > 0
        ).astype(jnp.bfloat16)
        covered *= 2
    return reach > 0


CHUNKS = 8


def project_kernel(attention_ref, weight_hbm, out_ref, weight_vmem, landed):
    rows = weight_vmem.shape[1]
    copies = [
        pltpu.make_async_copy(
            weight_hbm.at[pl.ds(chunk * rows, rows)], weight_vmem.at[chunk], landed.at[chunk]
        )
        for chunk in range(CHUNKS)
    ]
    for copy in copies:
        copy.start()
    attention = attention_ref[...]
    result = None
    for chunk in range(CHUNKS):
        copies[chunk].wait()
        part = jnp.dot(
            attention[:, chunk * rows : (chunk + 1) * rows],
            weight_vmem[chunk],
            preferred_element_type=jnp.float32,
        )
        result = part if result is None else result + part
    width = out_ref.shape[2]
    for piece in range(out_ref.shape[0]):
        out_ref[piece] = result[:, piece * width : (piece + 1) * width].astype(out_ref.dtype)


def project(attention, weight, pieces):
    rows, cols = weight.shape
    return pl.pallas_call(
        project_kernel,
        in_specs=[
            pl.BlockSpec(memory_space=pltpu.VMEM),
            pl.BlockSpec(memory_space=pl.ANY),
        ],
        out_specs=pl.BlockSpec(memory_space=pltpu.VMEM),
        out_shape=jax.ShapeDtypeStruct((pieces, attention.shape[0], cols // pieces), jnp.bfloat16),
        scratch_shapes=[
            pltpu.VMEM((CHUNKS, rows // CHUNKS, cols), weight.dtype),
            pltpu.SemaphoreType.DMA((CHUNKS,)),
        ],
    )(attention, weight)


def scale_heads(values, factors):
    return (values.reshape(factors.shape + (HD,)) * factors[..., None]).reshape(values.shape)


def on_device(
    queries,
    tree_keys,
    tree_values,
    cache_keys,
    cache_values,
    residual,
    out_weight,
    cache_len,
    parents,
    accept_rows,
    accept_len,
):
    member = lax.axis_index("mem")
    seq_rank = lax.axis_index("grp") * GROUP + member
    positions = cache_keys.shape[0]
    channels = cache_keys.shape[1]
    kv_local = channels // HD
    q_width = queries.shape[2]
    heads_local = q_width // HD
    sharing = heads_local // kv_local
    factor = 1.0 / math.sqrt(HD)
    regions = cache_len + A_MAX
    starts = jnp.cumsum(regions) - regions
    low_edge = seq_rank * positions
    places = low_edge + jnp.arange(positions, dtype=jnp.int32)

    sent = jnp.broadcast_to(queries, (GROUP,) + queries.shape[1:])
    keys_local = cache_keys.reshape(positions, kv_local, HD)
    values_local = cache_values.reshape(positions, kv_local, HD)
    gathered_q = lax.all_to_all(sent, "mem", 0, 0, tiled=True)

    group_base = seq_rank - member
    begin = lax.dynamic_slice_in_dim(starts, group_base, GROUP)
    length = lax.dynamic_slice_in_dim(cache_len, group_base, GROUP)
    inside = (places[None, :] >= begin[:, None]) & (places[None, :] < (begin + length)[:, None])
    shaped = gathered_q.reshape(GROUP, TREE, kv_local, sharing, HD)
    scores = (
        jnp.einsum("rtkgd,pkd->rkgtp", shaped, keys_local, preferred_element_type=jnp.float32)
        * factor
    )
    valid = inside[:, None, None, None, :]
    top_score = jnp.max(jnp.where(valid, scores, NEG), axis=-1)
    top_score = top_score.astype(jnp.bfloat16).astype(jnp.float32)
    raised = jnp.where(valid, jnp.exp(scores - top_score[..., None]), 0.0)
    total = jnp.sum(raised, axis=-1)
    summed = jnp.einsum(
        "rkgtp,pkd->rtkgd",
        raised.astype(jnp.bfloat16),
        values_local,
        preferred_element_type=jnp.float32,
    )
    stats = jnp.concatenate(
        [top_score.reshape(GROUP, 1, -1), total.reshape(GROUP, 1, -1)], axis=-1
    ).astype(jnp.bfloat16)
    stats = jnp.pad(stats, ((0, 0), (0, 0), (0, q_width - stats.shape[-1])))
    tree_pair = jnp.concatenate([tree_keys[0], tree_values[0]], axis=-1)
    mine_rows = jnp.take(tree_pair, accept_rows[0], axis=0)
    row_lines = mine_rows.reshape(1, -1, q_width)
    row_count = row_lines.shape[1]
    row_lines = jnp.broadcast_to(row_lines, (GROUP,) + row_lines.shape[1:])
    used = TREE + 1 + row_count
    filler = jnp.zeros((GROUP, -used % 16, q_width), jnp.bfloat16)
    message = jnp.concatenate(
        [summed.reshape(GROUP, TREE, q_width).astype(jnp.bfloat16), stats, row_lines, filler],
        axis=1,
    )
    message, queries, tree_keys, tree_values = lax.optimization_barrier(
        (message, queries, tree_keys, tree_values)
    )
    partials = lax.all_to_all(message, "mem", 0, 0, tiled=True)
    row_block = partials[:, TREE + 1 : used].reshape(GROUP, A_MAX, 2 * channels)
    partials = partials.astype(jnp.float32)
    part_out = partials[:, :TREE]
    stat_count = kv_local * sharing * TREE
    part_stats = partials[:, TREE, : 2 * stat_count].reshape(GROUP, 2, heads_local, TREE)
    part_top = jnp.transpose(part_stats[:, 0], (0, 2, 1))
    part_total = jnp.transpose(part_stats[:, 1], (0, 2, 1))

    linked = ancestry(parents[0])
    shaped_q = queries[0].reshape(TREE, kv_local, sharing, HD)
    own_keys = tree_keys[0].reshape(TREE, kv_local, HD)
    own_values = tree_values[0].reshape(TREE, kv_local, HD)
    drafted = (
        jnp.einsum("tkgd,jkd->kgtj", shaped_q, own_keys, preferred_element_type=jnp.float32)
        * factor
    )
    tree_top = jnp.max(jnp.where(linked, drafted, NEG), axis=-1)
    tree_raised = jnp.where(linked, jnp.exp(drafted - tree_top[..., None]), 0.0)
    tree_total = jnp.sum(tree_raised, axis=-1)
    tree_out = jnp.einsum(
        "kgtj,jkd->tkgd",
        tree_raised.astype(jnp.bfloat16),
        own_values,
        preferred_element_type=jnp.float32,
    ).reshape(TREE, q_width)
    tree_top = jnp.transpose(tree_top, (2, 0, 1)).reshape(TREE, heads_local)
    tree_total = jnp.transpose(tree_total, (2, 0, 1)).reshape(TREE, heads_local)

    joint_top = jnp.maximum(jnp.max(part_top, axis=0), tree_top)
    part_factor = jnp.exp(part_top - joint_top[None])
    tree_factor = jnp.exp(tree_top - joint_top)
    joint_out = jnp.sum(scale_heads(part_out, part_factor), axis=0) + scale_heads(
        tree_out, tree_factor
    )
    joint_total = jnp.sum(part_total * part_factor, axis=0) + tree_total * tree_factor
    attention = scale_heads(joint_out, 1.0 / joint_total).astype(jnp.bfloat16)

    tp_size = lax.axis_size("tp")
    projected = lax.dot_general(
        out_weight, attention, (((0,), (1,)), ((), ())), preferred_element_type=jnp.float32
    ).astype(jnp.bfloat16)
    pieces = projected.reshape(tp_size, -1, TREE)
    pieces = lax.all_to_all(pieces, "tp", 0, 0, tiled=True)
    summed_heads = jnp.sum(pieces.astype(jnp.float32), axis=0)
    mixed = (residual[0].astype(jnp.float32) + summed_heads.T).astype(jnp.bfloat16)[None]

    row_accepted = lax.dynamic_slice_in_dim(accept_len, group_base, GROUP)
    column = jnp.arange(A_MAX, dtype=jnp.int32)
    targets = begin[:, None] + length[:, None] + column[None, :] - low_edge
    keep_row = (column[None, :] < row_accepted[:, None]) & (targets >= 0) & (targets < positions)
    targets = jnp.where(keep_row, targets, positions).reshape(-1)
    rows = row_block.reshape(-1, 2 * channels)
    new_keys = cache_keys.at[targets].set(rows[:, :channels], mode="drop")
    new_values = cache_values.at[targets].set(rows[:, channels:], mode="drop")
    return (mixed, new_keys, new_values)


def solution(mesh):
    seq_size = mesh.shape["seq"]
    tp_size = mesh.shape["tp"]
    devices = np.asarray(mesh.devices).reshape(seq_size // GROUP, GROUP, tp_size)
    inner = Mesh(devices, ("grp", "mem", "tp"))
    seq = ("grp", "mem")
    return jax.shard_map(
        on_device,
        mesh=inner,
        in_specs=(
            P(seq, None, "tp"),
            P(seq, None, "tp"),
            P(seq, None, "tp"),
            P(seq, "tp"),
            P(seq, "tp"),
            P(seq, None, "tp"),
            P("tp", None),
            P(),
            P(seq, None),
            P(seq, None),
            P(),
        ),
        out_specs=(P(seq, None, "tp"), P(seq, "tp"), P(seq, "tp")),
        check_vma=False,
    )
```

```python
import math

import jax
import jax.numpy as jnp
import numpy as np
from jax import lax
from jax.experimental import pallas as pl
from jax.experimental.pallas import tpu as pltpu
from jax.sharding import Mesh
from jax.sharding import PartitionSpec as P

HD = 128
TREE = 32
A_MAX = 8
GROUP = 4


NEG = -1e30


def ancestry(parents):
    length = parents.shape[-1]
    members = jnp.arange(length, dtype=jnp.int32)
    step = (members[:, None] == members[None, :]) | (parents[:, None] == members[None, :])
    reach = step.astype(jnp.bfloat16)
    covered = 1
    while covered < length - 1:
        reach = (
            jnp.dot(reach, reach, preferred_element_type=jnp.float32) > 0
        ).astype(jnp.bfloat16)
        covered *= 2
    return reach > 0


CHUNKS = 8


def project_kernel(attention_ref, weight_hbm, out_ref, weight_vmem, landed):
    rows = weight_vmem.shape[1]
    copies = [
        pltpu.make_async_copy(
            weight_hbm.at[pl.ds(chunk * rows, rows)], weight_vmem.at[chunk], landed.at[chunk]
        )
        for chunk in range(CHUNKS)
    ]
    for copy in copies:
        copy.start()
    attention = attention_ref[...]
    result = None
    for chunk in range(CHUNKS):
        copies[chunk].wait()
        part = jnp.dot(
            attention[:, chunk * rows : (chunk + 1) * rows],
            weight_vmem[chunk],
            preferred_element_type=jnp.float32,
        )
        result = part if result is None else result + part
    width = out_ref.shape[2]
    for piece in range(out_ref.shape[0]):
        out_ref[piece] = result[:, piece * width : (piece + 1) * width].astype(out_ref.dtype)


def project(attention, weight, pieces):
    rows, cols = weight.shape
    return pl.pallas_call(
        project_kernel,
        in_specs=[
            pl.BlockSpec(memory_space=pltpu.VMEM),
            pl.BlockSpec(memory_space=pl.ANY),
        ],
        out_specs=pl.BlockSpec(memory_space=pltpu.VMEM),
        out_shape=jax.ShapeDtypeStruct((pieces, attention.shape[0], cols // pieces), jnp.bfloat16),
        scratch_shapes=[
            pltpu.VMEM((CHUNKS, rows // CHUNKS, cols), weight.dtype),
            pltpu.SemaphoreType.DMA((CHUNKS,)),
        ],
    )(attention, weight)


def scale_heads(values, factors):
    return (values.reshape(factors.shape + (HD,)) * factors[..., None]).reshape(values.shape)


def on_device(
    queries,
    tree_keys,
    tree_values,
    cache_keys,
    cache_values,
    residual,
    out_weight,
    cache_len,
    parents,
    accept_rows,
    accept_len,
):
    member = lax.axis_index("mem")
    seq_rank = lax.axis_index("grp") * GROUP + member
    positions = cache_keys.shape[0]
    channels = cache_keys.shape[1]
    kv_local = channels // HD
    q_width = queries.shape[2]
    heads_local = q_width // HD
    sharing = heads_local // kv_local
    factor = 1.0 / math.sqrt(HD)
    regions = cache_len + A_MAX
    low_edge = seq_rank * positions
    places = low_edge + jnp.arange(positions, dtype=jnp.int32)

    sent = jnp.broadcast_to(queries, (GROUP,) + queries.shape[1:])
    keys_local = cache_keys.reshape(positions, kv_local, HD)
    values_local = cache_values.reshape(positions, kv_local, HD)
    gathered_q = lax.all_to_all(sent, "mem", 0, 0, tiled=True)

    group_base = seq_rank - member
    owners = jnp.arange(cache_len.shape[0], dtype=jnp.int32)[None, :]
    wanted = group_base + jnp.arange(GROUP, dtype=jnp.int32)[:, None]
    begin = jnp.sum(jnp.where(owners < wanted, regions[None, :], 0), axis=1)
    length = jnp.sum(jnp.where(owners == wanted, cache_len[None, :], 0), axis=1)
    inside = (places[None, :] >= begin[:, None]) & (places[None, :] < (begin + length)[:, None])
    shaped = gathered_q.reshape(GROUP, TREE, kv_local, sharing, HD)
    scores = (
        jnp.einsum("rtkgd,pkd->rkgtp", shaped, keys_local, preferred_element_type=jnp.float32)
        * factor
    )
    valid = inside[:, None, None, None, :]
    top_score = jnp.max(jnp.where(valid, scores, NEG), axis=-1)
    top_score = top_score.astype(jnp.bfloat16).astype(jnp.float32)
    raised = jnp.where(valid, jnp.exp(scores - top_score[..., None]), 0.0)
    total = jnp.sum(raised, axis=-1)
    summed = jnp.einsum(
        "rkgtp,pkd->rtkgd",
        raised.astype(jnp.bfloat16),
        values_local,
        preferred_element_type=jnp.float32,
    )
    stats = jnp.concatenate(
        [top_score.reshape(GROUP, 1, -1), total.reshape(GROUP, 1, -1)], axis=-1
    ).astype(jnp.bfloat16)
    stats = jnp.pad(stats, ((0, 0), (0, 0), (0, q_width - stats.shape[-1])))
    chosen = (accept_rows.reshape(-1, 1) == jnp.arange(TREE, dtype=jnp.int32)[None, :]).astype(
        jnp.bfloat16
    )
    mine_rows = jnp.concatenate(
        [
            jnp.dot(chosen, tree_keys[0], preferred_element_type=jnp.float32),
            jnp.dot(chosen, tree_values[0], preferred_element_type=jnp.float32),
        ],
        axis=-1,
    ).astype(jnp.bfloat16)
    row_lines = mine_rows.reshape(1, -1, q_width)
    row_count = row_lines.shape[1]
    row_lines = jnp.broadcast_to(row_lines, (GROUP,) + row_lines.shape[1:])
    used = TREE + 1 + row_count
    filler = jnp.zeros((GROUP, -used % 16, q_width), jnp.bfloat16)
    message = jnp.concatenate(
        [summed.reshape(GROUP, TREE, q_width).astype(jnp.bfloat16), stats, row_lines, filler],
        axis=1,
    )
    message, queries, tree_keys, tree_values = lax.optimization_barrier(
        (message, queries, tree_keys, tree_values)
    )
    partials = lax.all_to_all(message, "mem", 0, 0, tiled=True)
    row_block = partials[:, TREE + 1 : used].reshape(GROUP, A_MAX, 2 * channels)
    partials = partials.astype(jnp.float32)
    part_out = partials[:, :TREE]
    stat_count = kv_local * sharing * TREE
    part_stats = partials[:, TREE, : 2 * stat_count].reshape(GROUP, 2, heads_local, TREE)
    part_top = jnp.transpose(part_stats[:, 0], (0, 2, 1))
    part_total = jnp.transpose(part_stats[:, 1], (0, 2, 1))

    linked = ancestry(parents[0])
    shaped_q = queries[0].reshape(TREE, kv_local, sharing, HD)
    own_keys = tree_keys[0].reshape(TREE, kv_local, HD)
    own_values = tree_values[0].reshape(TREE, kv_local, HD)
    drafted = (
        jnp.einsum("tkgd,jkd->kgtj", shaped_q, own_keys, preferred_element_type=jnp.float32)
        * factor
    )
    tree_top = jnp.max(jnp.where(linked, drafted, NEG), axis=-1)
    tree_raised = jnp.where(linked, jnp.exp(drafted - tree_top[..., None]), 0.0)
    tree_total = jnp.sum(tree_raised, axis=-1)
    tree_out = jnp.einsum(
        "kgtj,jkd->tkgd",
        tree_raised.astype(jnp.bfloat16),
        own_values,
        preferred_element_type=jnp.float32,
    ).reshape(TREE, q_width)
    tree_top = jnp.transpose(tree_top, (2, 0, 1)).reshape(TREE, heads_local)
    tree_total = jnp.transpose(tree_total, (2, 0, 1)).reshape(TREE, heads_local)

    joint_top = jnp.maximum(jnp.max(part_top, axis=0), tree_top)
    part_factor = jnp.exp(part_top - joint_top[None])
    tree_factor = jnp.exp(tree_top - joint_top)
    joint_out = jnp.sum(scale_heads(part_out, part_factor), axis=0) + scale_heads(
        tree_out, tree_factor
    )
    joint_total = jnp.sum(part_total * part_factor, axis=0) + tree_total * tree_factor
    attention = scale_heads(joint_out, 1.0 / joint_total).astype(jnp.bfloat16)

    tp_size = lax.axis_size("tp")
    projected = lax.dot_general(
        out_weight, attention, (((0,), (1,)), ((), ())), preferred_element_type=jnp.float32
    ).astype(jnp.bfloat16)
    pieces = projected.reshape(tp_size, -1, TREE)
    pieces = lax.all_to_all(pieces, "tp", 0, 0, tiled=True)
    summed_heads = jnp.sum(pieces.astype(jnp.float32), axis=0)
    mixed = (residual[0].astype(jnp.float32) + summed_heads.T).astype(jnp.bfloat16)[None]

    row_accepted = lax.dynamic_slice_in_dim(accept_len, group_base, GROUP)
    column = jnp.arange(A_MAX, dtype=jnp.int32)
    targets = begin[:, None] + length[:, None] + column[None, :] - low_edge
    keep_row = (column[None, :] < row_accepted[:, None]) & (targets >= 0) & (targets < positions)
    targets = jnp.where(keep_row, targets, positions).reshape(-1)
    rows = row_block.reshape(-1, 2 * channels)
    new_keys = cache_keys.at[targets].set(rows[:, :channels], mode="drop")
    new_values = cache_values.at[targets].set(rows[:, channels:], mode="drop")
    return (mixed, new_keys, new_values)


def solution(mesh):
    seq_size = mesh.shape["seq"]
    tp_size = mesh.shape["tp"]
    devices = np.asarray(mesh.devices).reshape(seq_size // GROUP, GROUP, tp_size)
    inner = Mesh(devices, ("grp", "mem", "tp"))
    seq = ("grp", "mem")
    return jax.shard_map(
        on_device,
        mesh=inner,
        in_specs=(
            P(seq, None, "tp"),
            P(seq, None, "tp"),
            P(seq, None, "tp"),
            P(seq, "tp"),
            P(seq, "tp"),
            P(seq, None, "tp"),
            P("tp", None),
            P(),
            P(seq, None),
            P(seq, None),
            P(),
        ),
        out_specs=(P(seq, None, "tp"), P(seq, "tp"), P(seq, "tp")),
        check_vma=False,
    )
```

```python
import math

import jax
import jax.numpy as jnp
import numpy as np
from jax import lax
from jax.experimental import pallas as pl
from jax.experimental.pallas import tpu as pltpu
from jax.sharding import Mesh
from jax.sharding import PartitionSpec as P

HD = 128
TREE = 32
A_MAX = 8
GROUP = 4


NEG = -1e30


def ancestry(parents):
    length = parents.shape[-1]
    members = jnp.arange(length, dtype=jnp.int32)
    step = (members[:, None] == members[None, :]) | (parents[:, None] == members[None, :])
    reach = step.astype(jnp.bfloat16)
    covered = 1
    while covered < length - 1:
        reach = (
            jnp.dot(reach, reach, preferred_element_type=jnp.float32) > 0
        ).astype(jnp.bfloat16)
        covered *= 2
    return reach > 0


CHUNKS = 8


def project_kernel(attention_ref, weight_hbm, out_ref, weight_vmem, landed):
    rows = weight_vmem.shape[1]
    copies = [
        pltpu.make_async_copy(
            weight_hbm.at[pl.ds(chunk * rows, rows)], weight_vmem.at[chunk], landed.at[chunk]
        )
        for chunk in range(CHUNKS)
    ]
    for copy in copies:
        copy.start()
    attention = attention_ref[...]
    result = None
    for chunk in range(CHUNKS):
        copies[chunk].wait()
        part = jnp.dot(
            attention[:, chunk * rows : (chunk + 1) * rows],
            weight_vmem[chunk],
            preferred_element_type=jnp.float32,
        )
        result = part if result is None else result + part
    width = out_ref.shape[2]
    for piece in range(out_ref.shape[0]):
        out_ref[piece] = result[:, piece * width : (piece + 1) * width].astype(out_ref.dtype)


def project(attention, weight, pieces):
    rows, cols = weight.shape
    return pl.pallas_call(
        project_kernel,
        in_specs=[
            pl.BlockSpec(memory_space=pltpu.VMEM),
            pl.BlockSpec(memory_space=pl.ANY),
        ],
        out_specs=pl.BlockSpec(memory_space=pltpu.VMEM),
        out_shape=jax.ShapeDtypeStruct((pieces, attention.shape[0], cols // pieces), jnp.bfloat16),
        scratch_shapes=[
            pltpu.VMEM((CHUNKS, rows // CHUNKS, cols), weight.dtype),
            pltpu.SemaphoreType.DMA((CHUNKS,)),
        ],
    )(attention, weight)


def scale_heads(values, factors):
    return (values.reshape(factors.shape + (HD,)) * factors[..., None]).reshape(values.shape)


def on_device(
    queries,
    tree_keys,
    tree_values,
    cache_keys,
    cache_values,
    residual,
    out_weight,
    cache_len,
    parents,
    accept_rows,
    accept_len,
):
    member = lax.axis_index("mem")
    seq_rank = lax.axis_index("grp") * GROUP + member
    positions = cache_keys.shape[0]
    channels = cache_keys.shape[1]
    kv_local = channels // HD
    q_width = queries.shape[2]
    heads_local = q_width // HD
    sharing = heads_local // kv_local
    factor = 1.0 / math.sqrt(HD)
    regions = cache_len + A_MAX
    low_edge = seq_rank * positions
    places = low_edge + jnp.arange(positions, dtype=jnp.int32)

    sent = jnp.broadcast_to(queries, (GROUP,) + queries.shape[1:])
    keys_local = cache_keys.reshape(positions, kv_local, HD)
    values_local = cache_values.reshape(positions, kv_local, HD)
    gathered_q = lax.all_to_all(sent, "mem", 0, 0, tiled=True)

    group_base = seq_rank - member
    owners = jnp.arange(cache_len.shape[0], dtype=jnp.int32)[None, :]
    wanted = group_base + jnp.arange(GROUP, dtype=jnp.int32)[:, None]
    begin = jnp.sum(jnp.where(owners < wanted, regions[None, :], 0), axis=1)
    length = jnp.sum(jnp.where(owners == wanted, cache_len[None, :], 0), axis=1)
    inside = (places[None, :] >= begin[:, None]) & (places[None, :] < (begin + length)[:, None])
    shaped = gathered_q.reshape(GROUP, TREE, kv_local, sharing, HD)
    scores = (
        jnp.einsum("rtkgd,pkd->rkgtp", shaped, keys_local, preferred_element_type=jnp.float32)
        * factor
    )
    valid = inside[:, None, None, None, :]
    top_score = jnp.max(jnp.where(valid, scores, NEG), axis=-1)
    top_score = top_score.astype(jnp.bfloat16).astype(jnp.float32)
    raised = jnp.where(valid, jnp.exp(scores - top_score[..., None]), 0.0)
    total = jnp.sum(raised, axis=-1)
    summed = jnp.einsum(
        "rkgtp,pkd->rtkgd",
        raised.astype(jnp.bfloat16),
        values_local,
        preferred_element_type=jnp.float32,
    )
    stats = jnp.concatenate(
        [top_score.reshape(GROUP, 1, -1), total.reshape(GROUP, 1, -1)], axis=-1
    ).astype(jnp.bfloat16)
    stats = jnp.pad(stats, ((0, 0), (0, 0), (0, q_width - stats.shape[-1])))
    chosen = (accept_rows.reshape(-1, 1) == jnp.arange(TREE, dtype=jnp.int32)[None, :]).astype(
        jnp.bfloat16
    )
    mine_rows = jnp.concatenate(
        [
            jnp.dot(chosen, tree_keys[0], preferred_element_type=jnp.float32),
            jnp.dot(chosen, tree_values[0], preferred_element_type=jnp.float32),
        ],
        axis=-1,
    ).astype(jnp.bfloat16)
    row_lines = mine_rows.reshape(1, -1, q_width)
    row_count = row_lines.shape[1]
    row_lines = jnp.broadcast_to(row_lines, (GROUP,) + row_lines.shape[1:])
    used = TREE + 1 + row_count
    filler = jnp.zeros((GROUP, -used % 16, q_width), jnp.bfloat16)
    message = jnp.concatenate(
        [summed.reshape(GROUP, TREE, q_width).astype(jnp.bfloat16), stats, row_lines, filler],
        axis=1,
    )
    message, queries, tree_keys, tree_values = lax.optimization_barrier(
        (message, queries, tree_keys, tree_values)
    )
    partials = lax.all_to_all(message, "mem", 0, 0, tiled=True)
    row_block = partials[:, TREE + 1 : used].reshape(GROUP, A_MAX, 2 * channels)
    partials = partials.astype(jnp.float32)
    part_out = partials[:, :TREE]
    stat_count = kv_local * sharing * TREE
    part_stats = partials[:, TREE, : 2 * stat_count].reshape(GROUP, 2, heads_local, TREE)
    part_top = jnp.transpose(part_stats[:, 0], (0, 2, 1))
    part_total = jnp.transpose(part_stats[:, 1], (0, 2, 1))

    linked = ancestry(parents[0])
    shaped_q = queries[0].reshape(TREE, kv_local, sharing, HD)
    own_keys = tree_keys[0].reshape(TREE, kv_local, HD)
    own_values = tree_values[0].reshape(TREE, kv_local, HD)
    drafted = (
        jnp.einsum("tkgd,jkd->kgtj", shaped_q, own_keys, preferred_element_type=jnp.float32)
        * factor
    )
    tree_top = jnp.max(jnp.where(linked, drafted, NEG), axis=-1)
    tree_raised = jnp.where(linked, jnp.exp(drafted - tree_top[..., None]), 0.0)
    tree_total = jnp.sum(tree_raised, axis=-1)
    tree_out = jnp.einsum(
        "kgtj,jkd->tkgd",
        tree_raised.astype(jnp.bfloat16),
        own_values,
        preferred_element_type=jnp.float32,
    ).reshape(TREE, q_width)
    tree_top = jnp.transpose(tree_top, (2, 0, 1)).reshape(TREE, heads_local)
    tree_total = jnp.transpose(tree_total, (2, 0, 1)).reshape(TREE, heads_local)

    joint_top = jnp.maximum(jnp.max(part_top, axis=0), tree_top)
    part_factor = jnp.exp(part_top - joint_top[None])
    tree_factor = jnp.exp(tree_top - joint_top)
    joint_out = jnp.sum(scale_heads(part_out, part_factor), axis=0) + scale_heads(
        tree_out, tree_factor
    )
    joint_total = jnp.sum(part_total * part_factor, axis=0) + tree_total * tree_factor
    attention = scale_heads(joint_out, 1.0 / joint_total).astype(jnp.bfloat16)

    tp_size = lax.axis_size("tp")
    pieces = lax.dot_general(
        out_weight.reshape(out_weight.shape[0], tp_size, -1),
        attention,
        (((0,), (1,)), ((), ())),
        preferred_element_type=jnp.float32,
    ).astype(jnp.bfloat16)
    pieces = lax.all_to_all(pieces, "tp", 0, 0, tiled=True)
    summed_heads = jnp.sum(pieces.astype(jnp.float32), axis=0)
    mixed = (residual[0].astype(jnp.float32) + summed_heads.T).astype(jnp.bfloat16)[None]

    row_accepted = lax.dynamic_slice_in_dim(accept_len, group_base, GROUP)
    column = jnp.arange(A_MAX, dtype=jnp.int32)
    targets = begin[:, None] + length[:, None] + column[None, :] - low_edge
    keep_row = (column[None, :] < row_accepted[:, None]) & (targets >= 0) & (targets < positions)
    targets = jnp.where(keep_row, targets, positions).reshape(-1)
    rows = row_block.reshape(-1, 2 * channels)
    new_keys = cache_keys.at[targets].set(rows[:, :channels], mode="drop")
    new_values = cache_values.at[targets].set(rows[:, channels:], mode="drop")
    return (mixed, new_keys, new_values)


def solution(mesh):
    seq_size = mesh.shape["seq"]
    tp_size = mesh.shape["tp"]
    devices = np.asarray(mesh.devices).reshape(seq_size // GROUP, GROUP, tp_size)
    inner = Mesh(devices, ("grp", "mem", "tp"))
    seq = ("grp", "mem")
    return jax.shard_map(
        on_device,
        mesh=inner,
        in_specs=(
            P(seq, None, "tp"),
            P(seq, None, "tp"),
            P(seq, None, "tp"),
            P(seq, "tp"),
            P(seq, "tp"),
            P(seq, None, "tp"),
            P("tp", None),
            P(),
            P(seq, None),
            P(seq, None),
            P(),
        ),
        out_specs=(P(seq, None, "tp"), P(seq, "tp"), P(seq, "tp")),
        check_vma=False,
    )
```

```python
import math

import jax
import jax.numpy as jnp
import numpy as np
from jax import lax
from jax.experimental import pallas as pl
from jax.experimental.pallas import tpu as pltpu
from jax.sharding import Mesh
from jax.sharding import PartitionSpec as P

HD = 128
TREE = 32
A_MAX = 8
GROUP = 4


NEG = -1e30


def ancestry(parents):
    length = parents.shape[-1]
    members = jnp.arange(length, dtype=jnp.int32)
    step = (members[:, None] == members[None, :]) | (parents[:, None] == members[None, :])
    reach = step.astype(jnp.bfloat16)
    covered = 1
    while covered < length - 1:
        reach = (
            jnp.dot(reach, reach, preferred_element_type=jnp.float32) > 0
        ).astype(jnp.bfloat16)
        covered *= 2
    return reach > 0


CHUNKS = 8


def project_kernel(attention_ref, weight_hbm, out_ref, weight_vmem, landed):
    rows = weight_vmem.shape[1]
    copies = [
        pltpu.make_async_copy(
            weight_hbm.at[pl.ds(chunk * rows, rows)], weight_vmem.at[chunk], landed.at[chunk]
        )
        for chunk in range(CHUNKS)
    ]
    for copy in copies:
        copy.start()
    attention = attention_ref[...]
    result = None
    for chunk in range(CHUNKS):
        copies[chunk].wait()
        part = jnp.dot(
            attention[:, chunk * rows : (chunk + 1) * rows],
            weight_vmem[chunk],
            preferred_element_type=jnp.float32,
        )
        result = part if result is None else result + part
    width = out_ref.shape[2]
    for piece in range(out_ref.shape[0]):
        out_ref[piece] = result[:, piece * width : (piece + 1) * width].astype(out_ref.dtype)


def project(attention, weight, pieces):
    rows, cols = weight.shape
    return pl.pallas_call(
        project_kernel,
        in_specs=[
            pl.BlockSpec(memory_space=pltpu.VMEM),
            pl.BlockSpec(memory_space=pl.ANY),
        ],
        out_specs=pl.BlockSpec(memory_space=pltpu.VMEM),
        out_shape=jax.ShapeDtypeStruct((pieces, attention.shape[0], cols // pieces), jnp.bfloat16),
        scratch_shapes=[
            pltpu.VMEM((CHUNKS, rows // CHUNKS, cols), weight.dtype),
            pltpu.SemaphoreType.DMA((CHUNKS,)),
        ],
    )(attention, weight)


def scale_heads(values, factors):
    return (values.reshape(factors.shape + (HD,)) * factors[..., None]).reshape(values.shape)


def on_device(
    queries,
    tree_keys,
    tree_values,
    cache_keys,
    cache_values,
    residual,
    out_weight,
    cache_len,
    parents,
    accept_rows,
    accept_len,
):
    member = lax.axis_index("mem")
    seq_rank = lax.axis_index("grp") * GROUP + member
    positions = cache_keys.shape[0]
    channels = cache_keys.shape[1]
    kv_local = channels // HD
    q_width = queries.shape[2]
    heads_local = q_width // HD
    sharing = heads_local // kv_local
    factor = 1.0 / math.sqrt(HD)
    regions = cache_len + A_MAX
    low_edge = seq_rank * positions
    places = low_edge + jnp.arange(positions, dtype=jnp.int32)

    sent = jnp.broadcast_to(queries, (GROUP,) + queries.shape[1:])
    keys_local = cache_keys.reshape(positions, kv_local, HD)
    values_local = cache_values.reshape(positions, kv_local, HD)
    gathered_q = lax.all_to_all(sent, "mem", 0, 0, tiled=True)

    group_base = seq_rank - member
    owners = jnp.arange(cache_len.shape[0], dtype=jnp.int32)[None, :]
    wanted = group_base + jnp.arange(GROUP, dtype=jnp.int32)[:, None]
    begin = jnp.sum(jnp.where(owners < wanted, regions[None, :], 0), axis=1)
    length = jnp.sum(jnp.where(owners == wanted, cache_len[None, :], 0), axis=1)
    inside = (places[None, :] >= begin[:, None]) & (places[None, :] < (begin + length)[:, None])
    shaped = gathered_q.reshape(GROUP, TREE, kv_local, sharing, HD)
    scores = (
        jnp.einsum("rtkgd,pkd->rkgtp", shaped, keys_local, preferred_element_type=jnp.float32)
        * factor
    )
    valid = inside[:, None, None, None, :]
    top_score = jnp.max(jnp.where(valid, scores, NEG), axis=-1)
    top_score = top_score.astype(jnp.bfloat16).astype(jnp.float32)
    raised = jnp.where(valid, jnp.exp(scores - top_score[..., None]), 0.0)
    total = jnp.sum(raised, axis=-1)
    summed = jnp.einsum(
        "rkgtp,pkd->rtkgd",
        raised.astype(jnp.bfloat16),
        values_local,
        preferred_element_type=jnp.float32,
    )
    stats = jnp.concatenate(
        [top_score.reshape(GROUP, 1, -1), total.reshape(GROUP, 1, -1)], axis=-1
    ).astype(jnp.bfloat16)
    stats = jnp.pad(stats, ((0, 0), (0, 0), (0, q_width - stats.shape[-1])))
    chosen = (accept_rows.reshape(-1, 1) == jnp.arange(TREE, dtype=jnp.int32)[None, :]).astype(
        jnp.bfloat16
    )
    mine_rows = jnp.concatenate(
        [
            jnp.dot(chosen, tree_keys[0], preferred_element_type=jnp.float32),
            jnp.dot(chosen, tree_values[0], preferred_element_type=jnp.float32),
        ],
        axis=-1,
    ).astype(jnp.bfloat16)
    row_lines = mine_rows.reshape(1, -1, q_width)
    row_count = row_lines.shape[1]
    row_lines = jnp.broadcast_to(row_lines, (GROUP,) + row_lines.shape[1:])
    used = TREE + 1 + row_count
    filler = jnp.zeros((GROUP, -used % 16, q_width), jnp.bfloat16)
    message = jnp.concatenate(
        [summed.reshape(GROUP, TREE, q_width).astype(jnp.bfloat16), stats, row_lines, filler],
        axis=1,
    )
    message, queries, tree_keys, tree_values = lax.optimization_barrier(
        (message, queries, tree_keys, tree_values)
    )
    partials = lax.all_to_all(message, "mem", 0, 0, tiled=True)
    row_block = partials[:, TREE + 1 : used].reshape(GROUP, A_MAX, 2 * channels)
    partials = partials.astype(jnp.float32)
    part_out = partials[:, :TREE]
    stat_count = kv_local * sharing * TREE
    part_stats = partials[:, TREE, : 2 * stat_count].reshape(GROUP, 2, heads_local, TREE)
    part_top = jnp.transpose(part_stats[:, 0], (0, 2, 1))
    part_total = jnp.transpose(part_stats[:, 1], (0, 2, 1))

    linked = ancestry(parents[0])
    shaped_q = queries[0].reshape(TREE, kv_local, sharing, HD)
    own_keys = tree_keys[0].reshape(TREE, kv_local, HD)
    own_values = tree_values[0].reshape(TREE, kv_local, HD)
    drafted = (
        jnp.einsum("tkgd,jkd->kgtj", shaped_q, own_keys, preferred_element_type=jnp.float32)
        * factor
    )
    tree_top = jnp.max(jnp.where(linked, drafted, NEG), axis=-1)
    tree_raised = jnp.where(linked, jnp.exp(drafted - tree_top[..., None]), 0.0)
    tree_total = jnp.sum(tree_raised, axis=-1)
    tree_out = jnp.einsum(
        "kgtj,jkd->tkgd",
        tree_raised.astype(jnp.bfloat16),
        own_values,
        preferred_element_type=jnp.float32,
    ).reshape(TREE, q_width)
    tree_top = jnp.transpose(tree_top, (2, 0, 1)).reshape(TREE, heads_local)
    tree_total = jnp.transpose(tree_total, (2, 0, 1)).reshape(TREE, heads_local)

    joint_top = jnp.maximum(jnp.max(part_top, axis=0), tree_top)
    part_factor = jnp.exp(part_top - joint_top[None])
    tree_factor = jnp.exp(tree_top - joint_top)
    joint_out = jnp.sum(scale_heads(part_out, part_factor), axis=0) + scale_heads(
        tree_out, tree_factor
    )
    joint_total = jnp.sum(part_total * part_factor, axis=0) + tree_total * tree_factor
    attention = scale_heads(joint_out, 1.0 / joint_total).astype(jnp.bfloat16)

    tp_size = lax.axis_size("tp")
    pieces = lax.dot_general(
        out_weight.reshape(out_weight.shape[0], tp_size, -1),
        attention,
        (((0,), (1,)), ((), ())),
        preferred_element_type=jnp.float32,
    ).astype(jnp.bfloat16)
    pieces = lax.all_to_all(pieces, "tp", 0, 0, tiled=True)
    summed_heads = jnp.sum(pieces.astype(jnp.float32), axis=0)
    mixed = (residual[0].astype(jnp.float32) + summed_heads.T).astype(jnp.bfloat16)[None]

    row_accepted = jnp.sum(jnp.where(owners == wanted, accept_len[None, :], 0), axis=1)
    offset = places[:, None] - (begin + length)[None, :]
    accepted = (offset >= 0) & (offset < row_accepted[None, :])
    slot = jnp.arange(GROUP * A_MAX, dtype=jnp.int32)[None, :]
    request_of = slot // A_MAX
    picked = jnp.zeros((positions, GROUP * A_MAX), dtype=jnp.bool_)
    for request in range(GROUP):
        picked = picked | (
            (request_of == request)
            & accepted[:, request : request + 1]
            & (offset[:, request : request + 1] == slot % A_MAX)
        )
    gathered = jnp.dot(
        picked.astype(jnp.bfloat16),
        row_block.reshape(GROUP * A_MAX, 2 * channels),
        preferred_element_type=jnp.float32,
    ).astype(jnp.bfloat16)
    matched = jnp.any(accepted, axis=1)[:, None]
    new_keys = jnp.where(matched, gathered[:, :channels], cache_keys)
    new_values = jnp.where(matched, gathered[:, channels:], cache_values)
    return (mixed, new_keys, new_values)


def solution(mesh):
    seq_size = mesh.shape["seq"]
    tp_size = mesh.shape["tp"]
    devices = np.asarray(mesh.devices).reshape(seq_size // GROUP, GROUP, tp_size)
    inner = Mesh(devices, ("grp", "mem", "tp"))
    seq = ("grp", "mem")
    return jax.shard_map(
        on_device,
        mesh=inner,
        in_specs=(
            P(seq, None, "tp"),
            P(seq, None, "tp"),
            P(seq, None, "tp"),
            P(seq, "tp"),
            P(seq, "tp"),
            P(seq, None, "tp"),
            P("tp", None),
            P(),
            P(seq, None),
            P(seq, None),
            P(),
        ),
        out_specs=(P(seq, None, "tp"), P(seq, "tp"), P(seq, "tp")),
        check_vma=False,
    )
```

```python
import math

import jax
import jax.numpy as jnp
import numpy as np
from jax import lax
from jax.experimental import pallas as pl
from jax.experimental.pallas import tpu as pltpu
from jax.sharding import Mesh
from jax.sharding import PartitionSpec as P

HD = 128
TREE = 32
A_MAX = 8
GROUP = 4


NEG = -1e30


def ancestry(parents):
    length = parents.shape[-1]
    members = jnp.arange(length, dtype=jnp.int32)
    step = (members[:, None] == members[None, :]) | (parents[:, None] == members[None, :])
    reach = step.astype(jnp.bfloat16)
    covered = 1
    while covered < length - 1:
        reach = (
            jnp.dot(reach, reach, preferred_element_type=jnp.float32) > 0
        ).astype(jnp.bfloat16)
        covered *= 2
    return reach > 0


CHUNKS = 8


def project_kernel(attention_ref, weight_hbm, out_ref, weight_vmem, landed):
    rows = weight_vmem.shape[1]
    copies = [
        pltpu.make_async_copy(
            weight_hbm.at[pl.ds(chunk * rows, rows)], weight_vmem.at[chunk], landed.at[chunk]
        )
        for chunk in range(CHUNKS)
    ]
    for copy in copies:
        copy.start()
    attention = attention_ref[...]
    result = None
    for chunk in range(CHUNKS):
        copies[chunk].wait()
        part = jnp.dot(
            attention[:, chunk * rows : (chunk + 1) * rows],
            weight_vmem[chunk],
            preferred_element_type=jnp.float32,
        )
        result = part if result is None else result + part
    width = out_ref.shape[2]
    for piece in range(out_ref.shape[0]):
        out_ref[piece] = result[:, piece * width : (piece + 1) * width].astype(out_ref.dtype)


def project(attention, weight, pieces):
    rows, cols = weight.shape
    return pl.pallas_call(
        project_kernel,
        in_specs=[
            pl.BlockSpec(memory_space=pltpu.VMEM),
            pl.BlockSpec(memory_space=pl.ANY),
        ],
        out_specs=pl.BlockSpec(memory_space=pltpu.VMEM),
        out_shape=jax.ShapeDtypeStruct((pieces, attention.shape[0], cols // pieces), jnp.bfloat16),
        scratch_shapes=[
            pltpu.VMEM((CHUNKS, rows // CHUNKS, cols), weight.dtype),
            pltpu.SemaphoreType.DMA((CHUNKS,)),
        ],
    )(attention, weight)


def scale_heads(values, factors):
    return (values.reshape(factors.shape + (HD,)) * factors[..., None]).reshape(values.shape)


def on_device(
    queries,
    tree_keys,
    tree_values,
    cache_keys,
    cache_values,
    residual,
    out_weight,
    cache_len,
    parents,
    accept_rows,
    accept_len,
):
    member = lax.axis_index("mem")
    seq_rank = lax.axis_index("grp") * GROUP + member
    positions = cache_keys.shape[0]
    channels = cache_keys.shape[1]
    kv_local = channels // HD
    q_width = queries.shape[2]
    heads_local = q_width // HD
    sharing = heads_local // kv_local
    factor = 1.0 / math.sqrt(HD)
    regions = cache_len + A_MAX
    low_edge = seq_rank * positions
    places = low_edge + jnp.arange(positions, dtype=jnp.int32)

    sent = jnp.broadcast_to(queries, (GROUP,) + queries.shape[1:])
    keys_local = cache_keys.reshape(positions, kv_local, HD)
    values_local = cache_values.reshape(positions, kv_local, HD)
    gathered_q = lax.all_to_all(sent, "mem", 0, 0, tiled=True)

    group_base = seq_rank - member
    owners = jnp.arange(cache_len.shape[0], dtype=jnp.int32)[None, :]
    wanted = group_base + jnp.arange(GROUP, dtype=jnp.int32)[:, None]
    begin = jnp.sum(jnp.where(owners < wanted, regions[None, :], 0), axis=1)
    length = jnp.sum(jnp.where(owners == wanted, cache_len[None, :], 0), axis=1)
    inside = (places[None, :] >= begin[:, None]) & (places[None, :] < (begin + length)[:, None])
    shaped = gathered_q.reshape(GROUP, TREE, kv_local, sharing, HD)
    scores = (
        jnp.einsum("rtkgd,pkd->rkgtp", shaped, keys_local, preferred_element_type=jnp.float32)
        * factor
    )
    valid = inside[:, None, None, None, :]
    top_score = jnp.max(jnp.where(valid, scores, NEG), axis=-1)
    top_score = top_score.astype(jnp.bfloat16).astype(jnp.float32)
    raised = jnp.where(valid, jnp.exp(scores - top_score[..., None]), 0.0)
    total = jnp.sum(raised, axis=-1)
    summed = jnp.einsum(
        "rkgtp,pkd->rtkgd",
        raised.astype(jnp.bfloat16),
        values_local,
        preferred_element_type=jnp.float32,
    )
    stats = jnp.concatenate(
        [top_score.reshape(GROUP, 1, -1), total.reshape(GROUP, 1, -1)], axis=-1
    ).astype(jnp.bfloat16)
    stats = jnp.pad(stats, ((0, 0), (0, 0), (0, q_width - stats.shape[-1])))
    chosen = (accept_rows.reshape(-1, 1) == jnp.arange(TREE, dtype=jnp.int32)[None, :]).astype(
        jnp.bfloat16
    )
    mine_rows = jnp.concatenate(
        [
            jnp.dot(chosen, tree_keys[0], preferred_element_type=jnp.float32),
            jnp.dot(chosen, tree_values[0], preferred_element_type=jnp.float32),
        ],
        axis=-1,
    ).astype(jnp.bfloat16)
    row_lines = mine_rows.reshape(1, -1, q_width)
    row_count = row_lines.shape[1]
    row_lines = jnp.broadcast_to(row_lines, (GROUP,) + row_lines.shape[1:])
    used = TREE + 1 + row_count
    filler = jnp.zeros((GROUP, -used % 16, q_width), jnp.bfloat16)
    message = jnp.concatenate(
        [summed.reshape(GROUP, TREE, q_width).astype(jnp.bfloat16), stats, row_lines, filler],
        axis=1,
    )
    message, queries, tree_keys, tree_values = lax.optimization_barrier(
        (message, queries, tree_keys, tree_values)
    )
    partials = lax.all_to_all(message, "mem", 0, 0, tiled=True)
    row_block = partials[:, TREE + 1 : used].reshape(GROUP, A_MAX, 2 * channels)
    partials = partials.astype(jnp.float32)
    part_out = partials[:, :TREE]
    stat_count = kv_local * sharing * TREE
    part_stats = partials[:, TREE, : 2 * stat_count].reshape(GROUP, 2, heads_local, TREE)
    part_top = part_stats[:, 0]
    part_total = part_stats[:, 1]

    linked = ancestry(parents[0])
    shaped_q = queries[0].reshape(TREE, kv_local, sharing, HD)
    own_keys = tree_keys[0].reshape(TREE, kv_local, HD)
    own_values = tree_values[0].reshape(TREE, kv_local, HD)
    drafted = (
        jnp.einsum("tkgd,jkd->kgtj", shaped_q, own_keys, preferred_element_type=jnp.float32)
        * factor
    )
    tree_top = jnp.max(jnp.where(linked, drafted, NEG), axis=-1)
    tree_raised = jnp.where(linked, jnp.exp(drafted - tree_top[..., None]), 0.0)
    tree_total = jnp.sum(tree_raised, axis=-1)
    tree_out = jnp.einsum(
        "kgtj,jkd->tkgd",
        tree_raised.astype(jnp.bfloat16),
        own_values,
        preferred_element_type=jnp.float32,
    ).reshape(TREE, q_width)
    tree_top = tree_top.reshape(heads_local, TREE)
    tree_total = tree_total.reshape(heads_local, TREE)

    joint_top = jnp.maximum(jnp.max(part_top, axis=0), tree_top)
    part_factor = jnp.exp(part_top - joint_top[None])
    tree_factor = jnp.exp(tree_top - joint_top)
    joint_total = jnp.sum(part_total * part_factor, axis=0) + tree_total * tree_factor
    part_factor = jnp.transpose(part_factor, (0, 2, 1))
    tree_factor = tree_factor.T
    joint_out = jnp.sum(scale_heads(part_out, part_factor), axis=0) + scale_heads(
        tree_out, tree_factor
    )
    attention = scale_heads(joint_out, 1.0 / joint_total.T).astype(jnp.bfloat16)

    tp_size = lax.axis_size("tp")
    pieces = lax.dot_general(
        out_weight.reshape(out_weight.shape[0], tp_size, -1),
        attention,
        (((0,), (1,)), ((), ())),
        preferred_element_type=jnp.float32,
    ).astype(jnp.bfloat16)
    pieces = lax.all_to_all(pieces, "tp", 0, 0, tiled=True)
    summed_heads = jnp.sum(pieces.astype(jnp.float32), axis=0)
    mixed = (residual[0].astype(jnp.float32) + summed_heads.T).astype(jnp.bfloat16)[None]

    row_accepted = jnp.sum(jnp.where(owners == wanted, accept_len[None, :], 0), axis=1)
    offset = places[:, None] - (begin + length)[None, :]
    accepted = (offset >= 0) & (offset < row_accepted[None, :])
    slot = jnp.arange(GROUP * A_MAX, dtype=jnp.int32)[None, :]
    request_of = slot // A_MAX
    picked = jnp.zeros((positions, GROUP * A_MAX), dtype=jnp.bool_)
    for request in range(GROUP):
        picked = picked | (
            (request_of == request)
            & accepted[:, request : request + 1]
            & (offset[:, request : request + 1] == slot % A_MAX)
        )
    gathered = jnp.dot(
        picked.astype(jnp.bfloat16),
        row_block.reshape(GROUP * A_MAX, 2 * channels),
        preferred_element_type=jnp.float32,
    ).astype(jnp.bfloat16)
    matched = jnp.any(accepted, axis=1)[:, None]
    new_keys = jnp.where(matched, gathered[:, :channels], cache_keys)
    new_values = jnp.where(matched, gathered[:, channels:], cache_values)
    return (mixed, new_keys, new_values)


def solution(mesh):
    seq_size = mesh.shape["seq"]
    tp_size = mesh.shape["tp"]
    devices = np.asarray(mesh.devices).reshape(seq_size // GROUP, GROUP, tp_size)
    inner = Mesh(devices, ("grp", "mem", "tp"))
    seq = ("grp", "mem")
    return jax.shard_map(
        on_device,
        mesh=inner,
        in_specs=(
            P(seq, None, "tp"),
            P(seq, None, "tp"),
            P(seq, None, "tp"),
            P(seq, "tp"),
            P(seq, "tp"),
            P(seq, None, "tp"),
            P("tp", None),
            P(),
            P(seq, None),
            P(seq, None),
            P(),
        ),
        out_specs=(P(seq, None, "tp"), P(seq, "tp"), P(seq, "tp")),
        check_vma=False,
    )
```
